32 devices in a mesh: ri: 4 (over z), ao: 8 (over y, x, core).
Axes of the slice: x: 2, y: 2, z: 4, core: 2. Of those that a mesh axis runs over, the one named last changes fastest.
Arguments:
- tensor: bfloat16 [512, 256, 256], P('ri', 'ao'), may hold values from -0.5 to 0.5
- live_blocks: int32 [8, 8, 8], P('ri', 'ao'), may hold values 0 or 1
- occ_density: bfloat16 [256, 256], P('ao'), may hold values from -0.375 to 0.375
- virt_density: bfloat16 [256, 256], P('ao'), may hold values from -0.375 to 0.375
- occ_mask: int32 [8, 8], P('ao'), may hold values 0 or 1
- virt_mask: int32 [8, 8], P('ao'), may hold values 0 or 1
- pair_slots: int32 [8, 8], P('ao'), may hold values from 0 to 7, as said below
Outputs:
- polar: float32 [512, 512], P('ri', 'ao')
The draws below stay inside these ranges and needn't reach their ends.
Inputs may be any that keep to these rules, and one draw needn't show every extreme that they name: pair_slots[b, 0] = b, and the 8 entries of a row are different AO blocks.
All inputs are finite; a program needn't handle non-finite values. No bound on the sum of `live_blocks` or of `occ_mask` or of `virt_mask` on one device may be relied on, other than what follows from the above.
Results may differ from the reference program's by a relative error of at most 0.0041.
Values may be sent and summed in bfloat16 or wider, within the bound.
No kernel may reach another device: no remote copies, remote signals or barrier semaphores. Data moves between devices by JAX's collectives and lax.ppermute only.
A program may use at most 192 MiB of HBM per device.

```python
import jax
import jax.numpy as jnp
from jax import lax

BS = 32
KS = 8
RB = 64
NRI = 512
NB = 8
NAO = 256


def draw_pair_slots(key, part):
    row_keys = jax.random.split(key, NB)

    def one_row(row_key, row_block):
        offsets = jax.random.permutation(row_key, NB - 1)[:KS - 1].astype(jnp.int32) + 1
        offsets = jnp.concatenate([jnp.zeros((1,), jnp.int32), offsets])
        return (row_block + offsets) % NB
    return jax.vmap(one_row)(row_keys, jnp.arange(NB, dtype=jnp.int32)).astype(jnp.int32)


def with_ends(drawn, rng, smallest, top_value):
    index_at = [jax.random.randint(jax.random.fold_in(rng, axis), (), 0, length) for axis, length in enumerate(drawn.shape)]
    main_axis = drawn.shape.index(max(drawn.shape))
    beside = index_at[:main_axis] + [(index_at[main_axis] + 1) % drawn.shape[main_axis]] + index_at[main_axis + 1:]
    return drawn.at[tuple(index_at)].set(smallest).at[tuple(beside)].set(top_value)


def shard_levels(own_key, dims, pieces, least, high):
    def one(dim, parts):
        steps = jax.random.uniform(jax.random.fold_in(jax.random.fold_in(own_key, 6), dim), (parts,), jnp.float32, least / len(pieces), high / len(pieces))
        return jnp.repeat(jnp.exp(steps), dims[dim] // parts).reshape((-1,) + (1,) * (len(dims) - dim - 1))

    level = one(*pieces[0])
    for cut in pieces[1:]:
        level = level * one(*cut)
    return level


def gaussian(own_key, shape, scale, reach, cuts=(), held_as=jnp.bfloat16):
    entries = scale * jax.random.normal(own_key, shape, jnp.float32)
    if cuts:
        entries = entries * shard_levels(own_key, shape, cuts, -0.22, 0.18)
    return jnp.clip(entries, -reach, reach).astype(held_as)


def setup_inputs(seed: int = 0) -> dict:
    key_list = jax.random.split(jax.random.key(seed), 8)
    return {
        "tensor": gaussian(key_list[0], (NRI, NAO, KS * BS), (4 * BS) ** -0.5, 0.5, ((0, 4), (1, 8))),
        "live_blocks": with_ends((jax.random.randint(key_list[1], (NRI // RB, NB, KS), 0, 4) < 3).astype(jnp.int32), jax.random.fold_in(key_list[1], 1), 0, 1),
        "occ_density": gaussian(key_list[2], (NAO, NAO), (KS * BS) ** -0.5, 0.375, ((0, 8),)),
        "virt_density": gaussian(key_list[3], (NAO, NAO), (KS * BS) ** -0.5, 0.375, ((0, 8),)),
        "occ_mask": with_ends((jax.random.randint(key_list[4], (NB, NB), 0, 4) < 3).astype(jnp.int32), jax.random.fold_in(key_list[4], 1), 0, 1),
        "virt_mask": with_ends((jax.random.randint(key_list[5], (NB, NB), 0, 4) < 3).astype(jnp.int32), jax.random.fold_in(key_list[5], 1), 0, 1),
        "pair_slots": draw_pair_slots(jax.random.fold_in(key_list[7], 71), 0),
    }


def screen_density(density, block_mask):
    block_total = block_mask.shape[0]
    shaped = density.reshape(block_total, BS, block_total, BS)
    keeper = block_mask.astype(density.dtype)[:, None, :, None]
    return (shaped * keeper).reshape(density.shape)


def reference(tensor, live_blocks, occ_density, virt_density, occ_mask, virt_mask, pair_slots):
    slab_rows = tensor.shape[0]
    ao_total = tensor.shape[1]
    block_total = ao_total // BS
    keeper = live_blocks.astype(tensor.dtype)[:, None, :, None, :, None]
    shaped = tensor.reshape(slab_rows // RB, RB, block_total, BS, KS, BS) * keeper
    tensor_five = shaped.reshape(slab_rows, block_total, BS, KS, BS).astype(jnp.float32)
    occ_eff = screen_density(occ_density, occ_mask).reshape(block_total, BS, ao_total)
    virt_eff = screen_density(virt_density, virt_mask).reshape(block_total, BS, ao_total)
    occ_rows = occ_eff[pair_slots].astype(jnp.float32)
    virt_rows = virt_eff[pair_slots].astype(jnp.float32)

    def per_block(running, block_index):
        occ_cols = lax.dynamic_slice_in_dim(occ_rows, block_index * BS, BS, 3)
        half_occ = jnp.einsum("pbikj,bkjl->lbip", tensor_five, occ_cols)
        half_occ = half_occ.astype(jnp.bfloat16).reshape(BS, ao_total, slab_rows)
        tensor_own = lax.dynamic_index_in_dim(tensor_five, block_index, 1, keepdims=False)
        virt_own = lax.dynamic_index_in_dim(virt_rows, block_index, 0, keepdims=False)
        half_virt = jnp.einsum("qikj,kjn->qin", tensor_own, virt_own).astype(jnp.bfloat16)
        added = jnp.einsum("lnp,qln->pq", half_occ.astype(jnp.float32), half_virt.astype(jnp.float32))
        return running + added, None

    polar, unused = lax.scan(per_block, jnp.zeros((slab_rows, slab_rows), jnp.float32),
                             jnp.arange(block_total, dtype=jnp.int32))
    return polar
```

```python
import jax
import jax.numpy as jnp
from jax import lax
from jax.sharding import PartitionSpec as P

BS = 32
KS = 8
RB = 64


def screen_density(density, block_mask):
    own_blocks = block_mask.shape[0]
    all_blocks = block_mask.shape[1]
    shaped = density.reshape(own_blocks, BS, all_blocks, BS)
    keeper = block_mask.astype(density.dtype)[:, None, :, None]
    return (shaped * keeper).reshape(density.shape)


def pair_routes(size):
    routes = []
    for dist in range(1, size // 2 + 1):
        if 2 * dist < size:
            route = [(r, (r + dist) % size) for r in range(size)]
        else:
            route = []
            for i in range(size // 2):
                if i % 2 == 0:
                    route.append((i, i + dist))
                else:
                    route.append((i + dist, i))
        partner = list(range(size))
        for src, dst in route:
            partner[dst] = src
        routes.append((route, partner))
    return routes


def half_products(slab, live, rhs):
    rows = slab.shape[0]
    groups = rows // RB
    keep = jnp.repeat(live[:, 0, :].astype(jnp.bfloat16), BS, axis=1)
    rhs_masked = rhs[None] * keep[:, None, :, None]
    shaped = slab.reshape(groups, RB * BS, KS * BS)
    out = jnp.einsum(
        "gmk,gdkl->gdml", shaped, rhs_masked, preferred_element_type=jnp.float32
    ).astype(jnp.bfloat16)
    ao_total = rhs.shape[2]
    occ_half = out[:, 0].reshape(rows, BS, ao_total)
    virt_half = out[:, 1].reshape(rows, BS, ao_total)
    return occ_half, virt_half


def swap_local(block, cycle_size):
    rows = block.shape[0]
    ao_total = block.shape[2]
    sent = block.reshape(rows, BS, cycle_size, BS).transpose(2, 0, 3, 1)
    got = lax.all_to_all(sent, "ao", 0, 0, tiled=True)
    return got.transpose(1, 2, 0, 3).reshape(rows, BS, ao_total)


def add_block(total, part, plane, col_block):
    rows = part.shape[0]
    at = (plane, jnp.int32(0), col_block * rows)
    here = lax.dynamic_slice(total, at, (1, rows, part.shape[1]))
    return lax.dynamic_update_slice(total, here + part[None], at)


def per_device(tensor, live_blocks, occ_density, virt_density, occ_mask, virt_mask, pair_slots):
    rows = tensor.shape[0]
    own_width = tensor.shape[1]
    assert own_width == BS
    planes = lax.axis_size("ri")
    cycle_size = lax.axis_size("ao")
    plane = lax.axis_index("ri")

    routes = pair_routes(planes)
    received = [
        (lax.ppermute(tensor, "ri", route), lax.ppermute(live_blocks, "ri", route), partner)
        for route, partner in routes
    ]

    stacked = jnp.stack(
        [screen_density(occ_density, occ_mask), screen_density(virt_density, virt_mask)]
    )
    full = lax.all_gather(stacked, "ao", axis=1, tiled=True)
    ao_total = full.shape[2]
    all_blocks = ao_total // BS
    picked = full.reshape(2, all_blocks, BS, ao_total)[:, pair_slots[0]]
    rhs = picked.reshape(2, KS * BS, ao_total)

    occ_own, virt_own = half_products(tensor, live_blocks, rhs)
    occ_own_t = swap_local(occ_own, cycle_size)
    virt_own_t = swap_local(virt_own, cycle_size)

    total = jnp.zeros((planes, rows, planes * rows), jnp.float32)
    diag = jnp.einsum("pln,qln->pq", occ_own_t, virt_own, preferred_element_type=jnp.float32)
    total = add_block(total, diag, plane, plane)
    for slab, live, partner in received:
        other = jnp.array(partner, jnp.int32)[plane]
        occ_other, virt_other = half_products(slab, live, rhs)
        mine_theirs = jnp.einsum(
            "pln,qln->pq", occ_own_t, virt_other, preferred_element_type=jnp.float32
        )
        theirs_mine = jnp.einsum(
            "pnl,qnl->pq", occ_other, virt_own_t, preferred_element_type=jnp.float32
        )
        total = add_block(total, mine_theirs, plane, other)
        total = add_block(total, theirs_mine, other, plane)

    in_plane = lax.psum_scatter(total, "ao", scatter_dimension=2, tiled=True)
    return lax.psum_scatter(in_plane, "ri", scatter_dimension=0, tiled=True)[0]


def solution(mesh):
    placed = (
        P("ri", "ao", None),
        P("ri", "ao", None),
        P("ao", None),
        P("ao", None),
        P("ao", None),
        P("ao", None),
        P("ao", None),
    )
    return jax.shard_map(
        per_device, mesh=mesh, in_specs=placed, out_specs=P("ri", "ao"), check_vma=False
    )
```

```python
import jax
import jax.numpy as jnp
from jax import lax
from jax.sharding import PartitionSpec as P

BS = 32
KS = 8
RB = 64


def screen_density(density, block_mask):
    own_blocks = block_mask.shape[0]
    all_blocks = block_mask.shape[1]
    shaped = density.reshape(own_blocks, BS, all_blocks, BS)
    keeper = block_mask.astype(density.dtype)[:, None, :, None]
    return (shaped * keeper).reshape(density.shape)


def pair_routes(size):
    routes = []
    for dist in range(1, size // 2 + 1):
        if 2 * dist < size:
            route = [(r, (r + dist) % size) for r in range(size)]
        else:
            route = []
            for i in range(size // 2):
                if i % 2 == 0:
                    route.append((i, i + dist))
                else:
                    route.append((i + dist, i))
        recv_from = list(range(size))
        send_to = list(range(size))
        for src, dst in route:
            recv_from[dst] = src
            send_to[src] = dst
        routes.append((route, recv_from, send_to))
    return routes


def mask_slab(slab, live):
    rows = slab.shape[0]
    groups = rows // RB
    keeper = live.astype(slab.dtype)[:, None, :, :, None]
    shaped = slab.reshape(groups, RB, slab.shape[1], KS, BS) * keeper
    return shaped.reshape(slab.shape)


def split_hi_lo(values):
    hi = values.astype(jnp.bfloat16)
    lo = (values - hi.astype(jnp.float32)).astype(jnp.bfloat16)
    return hi, lo


def slab_product(slab, hi, lo):
    flat = slab.reshape(slab.shape[0], -1)
    return jnp.dot(flat, hi, preferred_element_type=jnp.float32) + jnp.dot(
        flat, lo, preferred_element_type=jnp.float32
    )


def add_cols(total, part, col_block):
    rows = part.shape[0]
    at = (jnp.int32(0), col_block * rows)
    here = lax.dynamic_slice(total, at, part.shape)
    return lax.dynamic_update_slice(total, here + part, at)


def per_device(tensor, live_blocks, occ_density, virt_density, occ_mask, virt_mask, pair_slots):
    rows = tensor.shape[0]
    assert tensor.shape[1] == BS
    planes = lax.axis_size("ri")
    cycle_size = lax.axis_size("ao")
    plane = lax.axis_index("ri")

    routes = pair_routes(planes)
    received = [
        (lax.ppermute(tensor, "ri", route), lax.ppermute(live_blocks, "ri", route))
        for route, _, _ in routes
    ]

    stacked = jnp.stack(
        [screen_density(occ_density, occ_mask), screen_density(virt_density, virt_mask)]
    )
    full = lax.all_gather(stacked, "ao", axis=1, tiled=True)
    ao_total = full.shape[2]
    all_blocks = ao_total // BS
    picked = full.reshape(2, all_blocks, BS, ao_total)[:, pair_slots[0]]
    occ_rows = picked[0].reshape(KS * BS, ao_total)
    virt_rows = picked[1].reshape(KS * BS, ao_total)

    own = mask_slab(tensor, live_blocks)
    halves = jnp.einsum(
        "prk,dkc->dcrp",
        own,
        jnp.stack([occ_rows, virt_rows]),
        preferred_element_type=jnp.float32,
    ).astype(jnp.bfloat16)
    swapped = lax.all_to_all(halves, "ao", 1, 2, tiled=True)
    occ_t = swapped[0]
    virt_t = swapped[1]
    v_part = jnp.einsum("mn,lnp->lmp", virt_rows, occ_t, preferred_element_type=jnp.float32)
    w_part = jnp.einsum("kl,nlq->nkq", occ_rows, virt_t, preferred_element_type=jnp.float32)
    v_hi, v_lo = split_hi_lo(v_part.reshape(-1, rows))
    w_hi, w_lo = split_hi_lo(w_part.reshape(-1, rows))
    vw_hi = jnp.concatenate([v_hi, w_hi], axis=1)
    vw_lo = jnp.concatenate([v_lo, w_lo], axis=1)

    vw_hi, vw_lo, received = lax.optimization_barrier((vw_hi, vw_lo, received))
    total = jnp.zeros((rows, planes * rows), jnp.float32)
    total = add_cols(total, slab_product(own, w_hi, w_lo), plane)
    for (slab, live), (route, recv_from, send_to) in zip(received, routes):
        product = slab_product(mask_slab(slab, live), vw_hi, vw_lo)
        source = jnp.array(recv_from, jnp.int32)[plane]
        target = jnp.array(send_to, jnp.int32)[plane]
        total = add_cols(total, product[:, :rows].T, source)
        back = lax.ppermute(product[:, rows:], "ri", [(d, s) for s, d in route])
        total = add_cols(total, back, target)

    width = total.shape[1] // cycle_size
    sent = total.reshape(rows, cycle_size, width).transpose(1, 0, 2)
    got = lax.all_to_all(sent, "ao", 0, 0, tiled=True)
    return jnp.sum(got, axis=0)


def solution(mesh):
    placed = (
        P("ri", "ao", None),
        P("ri", "ao", None),
        P("ao", None),
        P("ao", None),
        P("ao", None),
        P("ao", None),
        P("ao", None),
    )
    return jax.shard_map(
        per_device, mesh=mesh, in_specs=placed, out_specs=P("ri", "ao"), check_vma=False
    )
```

```python
import jax
import jax.numpy as jnp
from jax import lax
from jax.sharding import PartitionSpec as P

BS = 32
KS = 8
RB = 64


def screen_density(density, block_mask):
    own_blocks = block_mask.shape[0]
    all_blocks = block_mask.shape[1]
    shaped = density.reshape(own_blocks, BS, all_blocks, BS)
    keeper = block_mask.astype(density.dtype)[:, None, :, None]
    return (shaped * keeper).reshape(density.shape)


def pair_routes(size):
    routes = []
    for dist in range(1, size // 2 + 1):
        if 2 * dist < size:
            route = [(r, (r + dist) % size) for r in range(size)]
        else:
            route = []
            for i in range(size // 2):
                if i % 2 == 0:
                    route.append((i, i + dist))
                else:
                    route.append((i + dist, i))
        recv_from = list(range(size))
        send_to = list(range(size))
        for src, dst in route:
            recv_from[dst] = src
            send_to[src] = dst
        routes.append((route, recv_from, send_to))
    return routes


def mask_slab(slab, live):
    keeper = jnp.repeat(jnp.repeat(live[:, 0, :].astype(slab.dtype), RB, axis=0), BS, axis=1)
    return slab * keeper[:, None, :]


def split_hi_lo(values):
    rounded = lax.reduce_precision(values, exponent_bits=8, mantissa_bits=7)
    return rounded.astype(jnp.bfloat16), (values - rounded).astype(jnp.bfloat16)


def slab_product(slab, hi, lo):
    flat = slab.reshape(slab.shape[0], -1)
    return jnp.dot(flat, hi, preferred_element_type=jnp.float32) + jnp.dot(
        flat, lo, preferred_element_type=jnp.float32
    )


def add_cols(total, part, col_block):
    rows = part.shape[0]
    at = (jnp.int32(0), col_block * rows)
    here = lax.dynamic_slice(total, at, part.shape)
    return lax.dynamic_update_slice(total, here + part, at)


def per_device(tensor, live_blocks, occ_density, virt_density, occ_mask, virt_mask, pair_slots):
    rows = tensor.shape[0]
    assert tensor.shape[1] == BS
    planes = lax.axis_size("ri")
    cycle_size = lax.axis_size("ao")
    plane = lax.axis_index("ri")

    routes = pair_routes(planes)
    own = mask_slab(tensor, live_blocks)
    received = [lax.ppermute(own, "ri", route) for route, _, _ in routes]

    stacked = jnp.stack(
        [screen_density(occ_density, occ_mask), screen_density(virt_density, virt_mask)]
    )
    full = lax.all_gather(stacked, "ao", axis=1, tiled=True)
    ao_total = full.shape[2]
    all_blocks = ao_total // BS
    picked = full.reshape(2, all_blocks, BS, ao_total)[:, pair_slots[0]]
    occ_rows = picked[0].reshape(KS * BS, ao_total)
    virt_rows = picked[1].reshape(KS * BS, ao_total)

    halves = jnp.einsum(
        "prk,dkc->dcrp",
        own,
        jnp.stack([occ_rows, virt_rows]),
        preferred_element_type=jnp.float32,
    ).astype(jnp.bfloat16)
    swapped = lax.all_to_all(halves, "ao", 1, 2, tiled=True)
    occ_t = swapped[0]
    virt_t = swapped[1]
    v_part = jnp.einsum("mn,lnp->lmp", virt_rows, occ_t, preferred_element_type=jnp.float32)
    w_part = jnp.einsum("kl,nlq->nkq", occ_rows, virt_t, preferred_element_type=jnp.float32)
    v_hi, v_lo = split_hi_lo(v_part.reshape(-1, rows))
    w_hi, w_lo = split_hi_lo(w_part.reshape(-1, rows))

    v_hi, v_lo, w_hi, w_lo, received = lax.optimization_barrier(
        (v_hi, v_lo, w_hi, w_lo, received)
    )
    total = jnp.zeros((rows, planes * rows), jnp.float32)
    total = add_cols(total, slab_product(own, w_hi, w_lo), plane)
    for slab, (route, recv_from, send_to) in zip(received, routes):
        source = jnp.array(recv_from, jnp.int32)[plane]
        target = jnp.array(send_to, jnp.int32)[plane]
        total = add_cols(total, slab_product(slab, v_hi, v_lo).T, source)
        back = lax.ppermute(slab_product(slab, w_hi, w_lo), "ri", [(d, s) for s, d in route])
        total = add_cols(total, back, target)

    width = total.shape[1] // cycle_size
    sent = total.reshape(rows, cycle_size, width).transpose(1, 0, 2)
    got = lax.all_to_all(sent, "ao", 0, 0, tiled=True)
    return jnp.sum(got, axis=0)


def solution(mesh):
    placed = (
        P("ri", "ao", None),
        P("ri", "ao", None),
        P("ao", None),
        P("ao", None),
        P("ao", None),
        P("ao", None),
        P("ao", None),
    )
    return jax.shard_map(
        per_device, mesh=mesh, in_specs=placed, out_specs=P("ri", "ao"), check_vma=False
    )
```

```python
import jax
import jax.numpy as jnp
from jax import lax
from jax.sharding import PartitionSpec as P

BS = 32
KS = 8
RB = 64


def screen_density(density, block_mask):
    own_blocks = block_mask.shape[0]
    all_blocks = block_mask.shape[1]
    shaped = density.reshape(own_blocks, BS, all_blocks, BS)
    keeper = block_mask.astype(density.dtype)[:, None, :, None]
    return (shaped * keeper).reshape(density.shape)


def pair_routes(size):
    routes = []
    for dist in range(1, size // 2 + 1):
        if 2 * dist < size:
            route = [(r, (r + dist) % size) for r in range(size)]
        else:
            route = []
            for i in range(size // 2):
                if i % 2 == 0:
                    route.append((i, i + dist))
                else:
                    route.append((i + dist, i))
        recv_from = list(range(size))
        send_to = list(range(size))
        for src, dst in route:
            recv_from[dst] = src
            send_to[src] = dst
        routes.append((route, recv_from, send_to))
    return routes


def mask_slab(slab, live):
    keeper = jnp.repeat(jnp.repeat(live[:, 0, :].astype(slab.dtype), RB, axis=0), BS, axis=1)
    return slab * keeper[:, None, :]


def split_hi_lo(values):
    rounded = lax.reduce_precision(values, exponent_bits=8, mantissa_bits=7)
    return rounded.astype(jnp.bfloat16), (values - rounded).astype(jnp.bfloat16)


def slab_product(slab, hi, lo):
    return jnp.einsum("srk,prk->sp", slab, hi, preferred_element_type=jnp.float32) + jnp.einsum(
        "srk,prk->sp", slab, lo, preferred_element_type=jnp.float32
    )


def add_cols(total, part, col_block):
    rows = part.shape[0]
    at = (jnp.int32(0), col_block * rows)
    here = lax.dynamic_slice(total, at, part.shape)
    return lax.dynamic_update_slice(total, here + part, at)


def per_device(tensor, live_blocks, occ_density, virt_density, occ_mask, virt_mask, pair_slots):
    rows = tensor.shape[0]
    assert tensor.shape[1] == BS
    planes = lax.axis_size("ri")
    cycle_size = lax.axis_size("ao")
    plane = lax.axis_index("ri")

    routes = pair_routes(planes)
    own = mask_slab(tensor, live_blocks)
    received = [lax.ppermute(own, "ri", route) for route, _, _ in routes]

    stacked = jnp.stack(
        [screen_density(occ_density, occ_mask), screen_density(virt_density, virt_mask)]
    )
    full = lax.all_gather(stacked, "ao", axis=1, tiled=True)
    ao_total = full.shape[2]
    all_blocks = ao_total // BS
    picked = full.reshape(2, all_blocks, BS, ao_total)[:, pair_slots[0]]
    occ_rows = picked[0].reshape(KS * BS, ao_total)
    virt_rows = picked[1].reshape(KS * BS, ao_total)

    halves = jnp.einsum(
        "prk,dkc->dcrp",
        own,
        jnp.stack([occ_rows, virt_rows]),
        preferred_element_type=jnp.float32,
    ).astype(jnp.bfloat16)
    swapped = lax.all_to_all(halves, "ao", 1, 2, tiled=True)
    occ_t = swapped[0]
    virt_t = swapped[1]
    v_part = jnp.einsum("mn,lnp->plm", virt_rows, occ_t, preferred_element_type=jnp.float32)
    w_part = jnp.einsum("kl,nlq->qnk", occ_rows, virt_t, preferred_element_type=jnp.float32)
    v_hi, v_lo = split_hi_lo(v_part)
    w_hi, w_lo = split_hi_lo(w_part)

    v_hi, v_lo, w_hi, w_lo, received = lax.optimization_barrier(
        (v_hi, v_lo, w_hi, w_lo, received)
    )
    total = jnp.zeros((rows, planes * rows), jnp.float32)
    total = add_cols(total, slab_product(own, w_hi, w_lo), plane)
    for slab, (route, recv_from, send_to) in zip(received, routes):
        source = jnp.array(recv_from, jnp.int32)[plane]
        target = jnp.array(send_to, jnp.int32)[plane]
        total = add_cols(total, slab_product(slab, v_hi, v_lo).T, source)
        back = lax.ppermute(slab_product(slab, w_hi, w_lo), "ri", [(d, s) for s, d in route])
        total = add_cols(total, back, target)

    width = total.shape[1] // cycle_size
    sent = total.reshape(rows, cycle_size, width).transpose(1, 0, 2)
    got = lax.all_to_all(sent, "ao", 0, 0, tiled=True)
    return jnp.sum(got, axis=0)


def solution(mesh):
    placed = (
        P("ri", "ao", None),
        P("ri", "ao", None),
        P("ao", None),
        P("ao", None),
        P("ao", None),
        P("ao", None),
        P("ao", None),
    )
    return jax.shard_map(
        per_device, mesh=mesh, in_specs=placed, out_specs=P("ri", "ao"), check_vma=False
    )
```

```python
import jax
import jax.numpy as jnp
from jax import lax
from jax.sharding import PartitionSpec as P

BS = 32
KS = 8
RB = 64


def screen_density(density, block_mask):
    own_blocks = block_mask.shape[0]
    all_blocks = block_mask.shape[1]
    shaped = density.reshape(own_blocks, BS, all_blocks, BS)
    keeper = block_mask.astype(density.dtype)[:, None, :, None]
    return (shaped * keeper).reshape(density.shape)


def pair_routes(size):
    routes = []
    for dist in range(1, size // 2 + 1):
        if 2 * dist < size:
            route = [(r, (r + dist) % size) for r in range(size)]
        else:
            route = []
            for i in range(size // 2):
                if i % 2 == 0:
                    route.append((i, i + dist))
                else:
                    route.append((i + dist, i))
        recv_from = list(range(size))
        send_to = list(range(size))
        for src, dst in route:
            recv_from[dst] = src
            send_to[src] = dst
        routes.append((route, recv_from, send_to))
    return routes


def mask_slab(slab, live):
    keeper = jnp.repeat(jnp.repeat(live[:, 0, :].astype(slab.dtype), RB, axis=0), BS, axis=1)
    return slab * keeper[:, None, :]


def split_hi_lo(values):
    rounded = lax.reduce_precision(values, exponent_bits=8, mantissa_bits=7)
    return rounded.astype(jnp.bfloat16), (values - rounded).astype(jnp.bfloat16)


def slab_product(flat, weights):
    out = jnp.dot(flat, weights, preferred_element_type=jnp.float32)
    half = weights.shape[1] // 2
    return out[:, :half] + out[:, half:]


def add_cols(total, part, col_block):
    rows = part.shape[0]
    at = (jnp.int32(0), col_block * rows)
    here = lax.dynamic_slice(total, at, part.shape)
    return lax.dynamic_update_slice(total, here + part, at)


def per_device(tensor, live_blocks, occ_density, virt_density, occ_mask, virt_mask, pair_slots):
    rows = tensor.shape[0]
    assert tensor.shape[1] == BS
    planes = lax.axis_size("ri")
    cycle_size = lax.axis_size("ao")
    plane = lax.axis_index("ri")

    routes = pair_routes(planes)
    own = mask_slab(tensor, live_blocks)
    own_flat = own.reshape(rows, -1)
    received = [lax.ppermute(own_flat, "ri", route) for route, _, _ in routes]

    stacked = jnp.stack(
        [screen_density(occ_density, occ_mask), screen_density(virt_density, virt_mask)]
    )
    full = lax.all_gather(stacked, "ao", axis=1, tiled=True)
    ao_total = full.shape[2]
    all_blocks = ao_total // BS
    picked = full.reshape(2, all_blocks, BS, ao_total)[:, pair_slots[0]]
    occ_rows = picked[0].reshape(KS * BS, ao_total)
    virt_rows = picked[1].reshape(KS * BS, ao_total)

    halves = jnp.einsum(
        "prk,dkc->dcrp",
        own,
        jnp.stack([occ_rows, virt_rows]),
        preferred_element_type=jnp.float32,
    ).astype(jnp.bfloat16)
    swapped = lax.all_to_all(halves, "ao", 1, 2, tiled=True)
    occ_t = swapped[0]
    virt_t = swapped[1]
    v_part = jnp.einsum("mn,lnp->plm", virt_rows, occ_t, preferred_element_type=jnp.float32)
    w_part = jnp.einsum("kl,nlq->qnk", occ_rows, virt_t, preferred_element_type=jnp.float32)
    v_hi, v_lo = split_hi_lo(v_part.reshape(rows, -1))
    w_hi, w_lo = split_hi_lo(w_part.reshape(rows, -1))
    v_weights = jnp.concatenate([v_hi, v_lo]).T
    w_weights = jnp.concatenate([w_hi, w_lo]).T
    diag = slab_product(own_flat, w_weights)

    v_weights, w_weights, diag, received = lax.optimization_barrier(
        (v_weights, w_weights, diag, received)
    )
    total = jnp.zeros((rows, planes * rows), jnp.float32)
    total = add_cols(total, diag, plane)
    for slab, (route, recv_from, send_to) in zip(received, routes):
        source = jnp.array(recv_from, jnp.int32)[plane]
        target = jnp.array(send_to, jnp.int32)[plane]
        total = add_cols(total, slab_product(slab, v_weights).T, source)
        back = lax.ppermute(slab_product(slab, w_weights), "ri", [(d, s) for s, d in route])
        total = add_cols(total, back, target)

    width = total.shape[1] // cycle_size
    sent = total.reshape(rows, cycle_size, width).transpose(1, 0, 2)
    got = lax.all_to_all(sent, "ao", 0, 0, tiled=True)
    return jnp.sum(got, axis=0)


def solution(mesh):
    placed = (
        P("ri", "ao", None),
        P("ri", "ao", None),
        P("ao", None),
        P("ao", None),
        P("ao", None),
        P("ao", None),
        P("ao", None),
    )
    return jax.shard_map(
        per_device, mesh=mesh, in_specs=placed, out_specs=P("ri", "ao"), check_vma=False
    )
```

```python
import jax
import jax.numpy as jnp
from jax import lax
from jax.sharding import PartitionSpec as P

BS = 32
KS = 8
RB = 64


def screen_density(density, block_mask):
    own_blocks = block_mask.shape[0]
    all_blocks = block_mask.shape[1]
    shaped = density.reshape(own_blocks, BS, all_blocks, BS)
    keeper = block_mask.astype(density.dtype)[:, None, :, None]
    return (shaped * keeper).reshape(density.shape)


def pair_routes(size):
    routes = []
    for dist in range(1, size // 2 + 1):
        if 2 * dist < size:
            route = [(r, (r + dist) % size) for r in range(size)]
        else:
            route = []
            for i in range(size // 2):
                if i % 2 == 0:
                    route.append((i, i + dist))
                else:
                    route.append((i + dist, i))
        recv_from = list(range(size))
        send_to = list(range(size))
        for src, dst in route:
            recv_from[dst] = src
            send_to[src] = dst
        routes.append((route, recv_from, send_to))
    return routes


def mask_slab(slab, live):
    keeper = jnp.repeat(jnp.repeat(live[:, 0, :].astype(slab.dtype), RB, axis=0), BS, axis=1)
    return slab * keeper[:, None, :]


def split_hi_lo(values):
    rounded = lax.reduce_precision(values, exponent_bits=8, mantissa_bits=7)
    return rounded.astype(jnp.bfloat16), (values - rounded).astype(jnp.bfloat16)


def slab_product(flat, weights):
    out = jnp.dot(flat, weights, preferred_element_type=jnp.float32)
    half = weights.shape[1] // 2
    return out[:, :half] + out[:, half:]


def gather_rows(block, cycle_size):
    me = lax.axis_index("ao")
    pieces = [block]
    for dist in range(1, cycle_size):
        route = [(i, (i + dist) % cycle_size) for i in range(cycle_size)]
        pieces.append(lax.ppermute(block, "ao", route))
    stacked = jnp.stack(pieces)
    order = (me - jnp.arange(cycle_size, dtype=jnp.int32)) % cycle_size
    got = jnp.take(stacked, order, axis=0)
    return jnp.moveaxis(got, 0, 1).reshape(
        block.shape[0], cycle_size * block.shape[1], block.shape[2]
    )


def swap_blocks(halves, cycle_size):
    me = lax.axis_index("ao")
    width = halves.shape[1] // cycle_size
    pieces = []
    for dist in range(cycle_size):
        start = ((me + dist) % cycle_size) * width
        piece = lax.dynamic_slice_in_dim(halves, start, width, axis=1)
        if dist:
            route = [(i, (i + dist) % cycle_size) for i in range(cycle_size)]
            piece = lax.ppermute(piece, "ao", route)
        pieces.append(piece)
    stacked = jnp.stack(pieces)
    order = (me - jnp.arange(cycle_size, dtype=jnp.int32)) % cycle_size
    got = jnp.take(stacked, order, axis=0)
    return jnp.moveaxis(got, 0, 2).reshape(
        halves.shape[0], width, cycle_size * halves.shape[2], halves.shape[3]
    )


def add_cols(total, part, col_block):
    rows = part.shape[0]
    at = (jnp.int32(0), col_block * rows)
    here = lax.dynamic_slice(total, at, part.shape)
    return lax.dynamic_update_slice(total, here + part, at)


def per_device(tensor, live_blocks, occ_density, virt_density, occ_mask, virt_mask, pair_slots):
    rows = tensor.shape[0]
    assert tensor.shape[1] == BS
    planes = lax.axis_size("ri")
    cycle_size = lax.axis_size("ao")
    plane = lax.axis_index("ri")

    routes = pair_routes(planes)
    own = mask_slab(tensor, live_blocks)
    own_flat = own.reshape(rows, -1)
    received = [lax.ppermute(own_flat, "ri", route) for route, _, _ in routes]

    stacked = jnp.stack(
        [screen_density(occ_density, occ_mask), screen_density(virt_density, virt_mask)]
    )
    full = gather_rows(stacked, cycle_size)
    ao_total = full.shape[2]
    all_blocks = ao_total // BS
    picked = full.reshape(2, all_blocks, BS, ao_total)[:, pair_slots[0]]
    occ_rows = picked[0].reshape(KS * BS, ao_total)
    virt_rows = picked[1].reshape(KS * BS, ao_total)

    halves = jnp.einsum(
        "prk,dkc->dcrp",
        own,
        jnp.stack([occ_rows, virt_rows]),
        preferred_element_type=jnp.float32,
    ).astype(jnp.bfloat16)
    swapped = swap_blocks(halves, cycle_size)
    occ_t = swapped[0]
    virt_t = swapped[1]
    v_part = jnp.einsum("mn,lnp->plm", virt_rows, occ_t, preferred_element_type=jnp.float32)
    w_part = jnp.einsum("kl,nlq->qnk", occ_rows, virt_t, preferred_element_type=jnp.float32)
    v_hi, v_lo = split_hi_lo(v_part.reshape(rows, -1))
    w_hi, w_lo = split_hi_lo(w_part.reshape(rows, -1))
    v_weights = jnp.concatenate([v_hi, v_lo]).T
    w_weights = jnp.concatenate([w_hi, w_lo]).T
    diag = slab_product(own_flat, w_weights)

    v_weights, w_weights, diag, received = lax.optimization_barrier(
        (v_weights, w_weights, diag, received)
    )
    total = jnp.zeros((rows, planes * rows), jnp.float32)
    total = add_cols(total, diag, plane)
    for slab, (route, recv_from, send_to) in zip(received, routes):
        source = jnp.array(recv_from, jnp.int32)[plane]
        target = jnp.array(send_to, jnp.int32)[plane]
        total = add_cols(total, slab_product(slab, v_weights).T, source)
        back = lax.ppermute(slab_product(slab, w_weights), "ri", [(d, s) for s, d in route])
        total = add_cols(total, back, target)

    width = total.shape[1] // cycle_size
    sent = total.reshape(rows, cycle_size, width).transpose(1, 0, 2)
    got = lax.all_to_all(sent, "ao", 0, 0, tiled=True)
    return jnp.sum(got, axis=0)


def solution(mesh):
    placed = (
        P("ri", "ao", None),
        P("ri", "ao", None),
        P("ao", None),
        P("ao", None),
        P("ao", None),
        P("ao", None),
        P("ao", None),
    )
    return jax.shard_map(
        per_device, mesh=mesh, in_specs=placed, out_specs=P("ri", "ao"), check_vma=False
    )
```

```python
import jax
import jax.numpy as jnp
from jax import lax
from jax.sharding import PartitionSpec as P

BS = 32
KS = 8
RB = 64


def screen_density(density, block_mask):
    own_blocks = block_mask.shape[0]
    all_blocks = block_mask.shape[1]
    shaped = density.reshape(own_blocks, BS, all_blocks, BS)
    keeper = block_mask.astype(density.dtype)[:, None, :, None]
    return (shaped * keeper).reshape(density.shape)


def pair_routes(size):
    routes = []
    for dist in range(1, size // 2 + 1):
        if 2 * dist < size:
            route = [(r, (r + dist) % size) for r in range(size)]
        else:
            route = []
            for i in range(size // 2):
                if i % 2 == 0:
                    route.append((i, i + dist))
                else:
                    route.append((i + dist, i))
        recv_from = list(range(size))
        send_to = list(range(size))
        for src, dst in route:
            recv_from[dst] = src
            send_to[src] = dst
        routes.append((route, recv_from, send_to))
    return routes


def mask_slab(slab, live):
    keeper = jnp.repeat(jnp.repeat(live[:, 0, :].astype(slab.dtype), RB, axis=0), BS, axis=1)
    return slab * keeper[:, None, :]


def split_hi_lo(values):
    rounded = lax.reduce_precision(values, exponent_bits=8, mantissa_bits=7)
    return rounded.astype(jnp.bfloat16), (values - rounded).astype(jnp.bfloat16)


def weight_pair(values):
    hi, lo = split_hi_lo(values)
    return jnp.stack([hi, lo], axis=1).reshape(values.shape[0], -1)


def slab_product(flat, weights):
    out = jnp.dot(flat, weights, preferred_element_type=jnp.float32)
    half = weights.shape[1] // 2
    return out[:, :half] + out[:, half:]


def add_cols(total, part, col_block):
    rows = part.shape[0]
    at = (jnp.int32(0), col_block * rows)
    here = lax.dynamic_slice(total, at, part.shape)
    return lax.dynamic_update_slice(total, here + part, at)


def per_device(tensor, live_blocks, occ_density, virt_density, occ_mask, virt_mask, pair_slots):
    rows = tensor.shape[0]
    assert tensor.shape[1] == BS
    planes = lax.axis_size("ri")
    cycle_size = lax.axis_size("ao")
    plane = lax.axis_index("ri")

    routes = pair_routes(planes)
    own = mask_slab(tensor, live_blocks)
    own_flat = own.transpose(0, 2, 1).reshape(rows, -1)
    received = [lax.ppermute(own_flat, "ri", route) for route, _, _ in routes]

    stacked = jnp.stack(
        [screen_density(occ_density, occ_mask), screen_density(virt_density, virt_mask)]
    )
    full = lax.all_gather(stacked, "ao", axis=1, tiled=True)
    ao_total = full.shape[2]
    all_blocks = ao_total // BS
    picked = full.reshape(2, all_blocks, BS, ao_total)[:, pair_slots[0]]
    occ_rows = picked[0].reshape(KS * BS, ao_total)
    virt_rows = picked[1].reshape(KS * BS, ao_total)

    halves = jnp.einsum(
        "dkc,prk->dcpr",
        jnp.stack([occ_rows, virt_rows]),
        own,
        preferred_element_type=jnp.float32,
    ).astype(jnp.bfloat16)
    swapped = lax.all_to_all(halves, "ao", 1, 3, tiled=True)
    occ_t = swapped[0]
    virt_t = swapped[1]
    v_part = jnp.einsum("mn,lpn->mlp", virt_rows, occ_t, preferred_element_type=jnp.float32)
    w_part = jnp.einsum("kl,nql->knq", occ_rows, virt_t, preferred_element_type=jnp.float32)
    v_weights = weight_pair(v_part.reshape(-1, rows))
    w_weights = weight_pair(w_part.reshape(-1, rows))
    diag = slab_product(own_flat, w_weights)

    v_weights, w_weights, diag, received = lax.optimization_barrier(
        (v_weights, w_weights, diag, received)
    )
    total = jnp.zeros((rows, planes * rows), jnp.float32)
    total = add_cols(total, diag, plane)
    for slab, (route, recv_from, send_to) in zip(received, routes):
        source = jnp.array(recv_from, jnp.int32)[plane]
        target = jnp.array(send_to, jnp.int32)[plane]
        total = add_cols(total, slab_product(slab, v_weights).T, source)
        back = lax.ppermute(slab_product(slab, w_weights), "ri", [(d, s) for s, d in route])
        total = add_cols(total, back, target)

    width = total.shape[1] // cycle_size
    sent = total.reshape(rows, cycle_size, width).transpose(1, 0, 2)
    got = lax.all_to_all(sent, "ao", 0, 0, tiled=True)
    return jnp.sum(got, axis=0)


def solution(mesh):
    placed = (
        P("ri", "ao", None),
        P("ri", "ao", None),
        P("ao", None),
        P("ao", None),
        P("ao", None),
        P("ao", None),
        P("ao", None),
    )
    return jax.shard_map(
        per_device, mesh=mesh, in_specs=placed, out_specs=P("ri", "ao"), check_vma=False
    )
```

```python
import jax
import jax.numpy as jnp
from jax import lax
from jax.sharding import PartitionSpec as P

BS = 32
KS = 8
RB = 64


def screen_density(density, block_mask):
    own_blocks = block_mask.shape[0]
    all_blocks = block_mask.shape[1]
    shaped = density.reshape(own_blocks, BS, all_blocks, BS)
    keeper = block_mask.astype(density.dtype)[:, None, :, None]
    return (shaped * keeper).reshape(density.shape)


def pair_routes(size):
    routes = []
    for dist in range(1, size // 2 + 1):
        if 2 * dist < size:
            route = [(r, (r + dist) % size) for r in range(size)]
        else:
            route = []
            for i in range(size // 2):
                if i % 2 == 0:
                    route.append((i, i + dist))
                else:
                    route.append((i + dist, i))
        recv_from = list(range(size))
        send_to = list(range(size))
        for src, dst in route:
            recv_from[dst] = src
            send_to[src] = dst
        routes.append((route, recv_from, send_to))
    return routes


def mask_slab(slab, live):
    keeper = jnp.repeat(jnp.repeat(live[:, 0, :].astype(slab.dtype), RB, axis=0), BS, axis=1)
    return slab * keeper[:, None, :]


def split_hi_lo(values):
    rounded = lax.reduce_precision(values, exponent_bits=8, mantissa_bits=7)
    return rounded.astype(jnp.bfloat16), (values - rounded).astype(jnp.bfloat16)


def slab_product(flat, weights):
    out = jnp.dot(flat, weights, preferred_element_type=jnp.float32)
    half = weights.shape[1] // 2
    return out[:, :half] + out[:, half:]


def add_cols(total, part, col_block):
    rows = part.shape[0]
    at = (jnp.int32(0), col_block * rows)
    here = lax.dynamic_slice(total, at, part.shape)
    return lax.dynamic_update_slice(total, here + part, at)


def per_device(tensor, live_blocks, occ_density, virt_density, occ_mask, virt_mask, pair_slots):
    rows = tensor.shape[0]
    assert tensor.shape[1] == BS
    planes = lax.axis_size("ri")
    cycle_size = lax.axis_size("ao")
    plane = lax.axis_index("ri")

    routes = pair_routes(planes)
    own = mask_slab(tensor, live_blocks)
    own_flat = own.reshape(rows, -1)
    lead = rows // 4
    early = [lax.ppermute(own_flat[:lead], "ri", route) for route, _, _ in routes]
    late = [lax.ppermute(own_flat[lead:], "ri", route) for route, _, _ in routes]

    stacked = jnp.stack(
        [screen_density(occ_density, occ_mask), screen_density(virt_density, virt_mask)]
    )
    full = lax.all_gather(stacked, "ao", axis=1, tiled=True)
    ao_total = full.shape[2]
    all_blocks = ao_total // BS
    picked = full.reshape(2, all_blocks, BS, ao_total)[:, pair_slots[0]]
    occ_rows = picked[0].reshape(KS * BS, ao_total)
    virt_rows = picked[1].reshape(KS * BS, ao_total)

    halves = jnp.einsum(
        "prk,dkc->dcrp",
        own,
        jnp.stack([occ_rows, virt_rows]),
        preferred_element_type=jnp.float32,
    ).astype(jnp.bfloat16)
    halves, early = lax.optimization_barrier((halves, early))
    swapped = lax.all_to_all(halves, "ao", 1, 2, tiled=True)
    occ_t = swapped[0]
    virt_t = swapped[1]
    v_part = jnp.einsum("mn,lnp->plm", virt_rows, occ_t, preferred_element_type=jnp.float32)
    w_part = jnp.einsum("kl,nlq->qnk", occ_rows, virt_t, preferred_element_type=jnp.float32)
    v_hi, v_lo = split_hi_lo(v_part.reshape(rows, -1))
    w_hi, w_lo = split_hi_lo(w_part.reshape(rows, -1))
    v_weights = jnp.concatenate([v_hi, v_lo]).T
    w_weights = jnp.concatenate([w_hi, w_lo]).T
    diag = slab_product(own_flat, w_weights)

    v_weights, w_weights, diag, late = lax.optimization_barrier(
        (v_weights, w_weights, diag, late)
    )
    received = [jnp.concatenate([a, b]) for a, b in zip(early, late)]
    total = jnp.zeros((rows, planes * rows), jnp.float32)
    total = add_cols(total, diag, plane)
    for slab, (route, recv_from, send_to) in zip(received, routes):
        source = jnp.array(recv_from, jnp.int32)[plane]
        target = jnp.array(send_to, jnp.int32)[plane]
        total = add_cols(total, slab_product(slab, v_weights).T, source)
        back = lax.ppermute(slab_product(slab, w_weights), "ri", [(d, s) for s, d in route])
        total = add_cols(total, back, target)

    width = total.shape[1] // cycle_size
    sent = total.reshape(rows, cycle_size, width).transpose(1, 0, 2)
    got = lax.all_to_all(sent, "ao", 0, 0, tiled=True)
    return jnp.sum(got, axis=0)


def solution(mesh):
    placed = (
        P("ri", "ao", None),
        P("ri", "ao", None),
        P("ao", None),
        P("ao", None),
        P("ao", None),
        P("ao", None),
        P("ao", None),
    )
    return jax.shard_map(
        per_device, mesh=mesh, in_specs=placed, out_specs=P("ri", "ao"), check_vma=False
    )
```

```python
import jax
import jax.numpy as jnp
from jax import lax
from jax.sharding import PartitionSpec as P

BS = 32
KS = 8
RB = 64


def screen_density(density, block_mask):
    own_blocks = block_mask.shape[0]
    all_blocks = block_mask.shape[1]
    shaped = density.reshape(own_blocks, BS, all_blocks, BS)
    keeper = block_mask.astype(density.dtype)[:, None, :, None]
    return (shaped * keeper).reshape(density.shape)


def pair_routes(size):
    routes = []
    for dist in range(1, size // 2 + 1):
        if 2 * dist < size:
            route = [(r, (r + dist) % size) for r in range(size)]
        else:
            route = []
            for i in range(size // 2):
                if i % 2 == 0:
                    route.append((i, i + dist))
                else:
                    route.append((i + dist, i))
        recv_from = list(range(size))
        send_to = list(range(size))
        for src, dst in route:
            recv_from[dst] = src
            send_to[src] = dst
        routes.append((route, recv_from, send_to))
    return routes


def mask_slab(slab, live):
    keeper = jnp.repeat(jnp.repeat(live[:, 0, :].astype(slab.dtype), RB, axis=0), BS, axis=1)
    return slab * keeper[:, None, :]


def split_hi_lo(values):
    rounded = lax.reduce_precision(values, exponent_bits=8, mantissa_bits=7)
    return rounded.astype(jnp.bfloat16), (values - rounded).astype(jnp.bfloat16)


def weight_pair(values):
    hi, lo = split_hi_lo(values)
    both = jnp.stack([hi, lo])
    return both.transpose(2, 3, 0, 1).reshape(values.shape[1] * values.shape[2], -1)


def slab_product(flat, weights):
    out = jnp.dot(flat, weights, preferred_element_type=jnp.float32)
    half = weights.shape[1] // 2
    return out[:, :half] + out[:, half:]


def add_cols(total, part, col_block):
    rows = part.shape[0]
    at = (jnp.int32(0), col_block * rows)
    here = lax.dynamic_slice(total, at, part.shape)
    return lax.dynamic_update_slice(total, here + part, at)


def per_device(tensor, live_blocks, occ_density, virt_density, occ_mask, virt_mask, pair_slots):
    rows = tensor.shape[0]
    assert tensor.shape[1] == BS
    planes = lax.axis_size("ri")
    cycle_size = lax.axis_size("ao")
    plane = lax.axis_index("ri")

    routes = pair_routes(planes)
    own = mask_slab(tensor, live_blocks)
    own_flat = own.reshape(rows, -1)
    lead = rows // 4
    early = [lax.ppermute(own_flat[:lead], "ri", route) for route, _, _ in routes]
    late = [lax.ppermute(own_flat[lead:], "ri", route) for route, _, _ in routes]

    stacked = jnp.stack(
        [screen_density(occ_density, occ_mask), screen_density(virt_density, virt_mask)]
    )
    full = lax.all_gather(stacked, "ao", axis=1, tiled=True)
    ao_total = full.shape[2]
    all_blocks = ao_total // BS
    picked = full.reshape(2, all_blocks, BS, ao_total)[:, pair_slots[0]]
    occ_rows = picked[0].reshape(KS * BS, ao_total)
    virt_rows = picked[1].reshape(KS * BS, ao_total)

    halves = jnp.einsum(
        "prk,dkc->dcrp",
        own,
        jnp.stack([occ_rows, virt_rows]),
        preferred_element_type=jnp.float32,
    ).astype(jnp.bfloat16)
    halves, early = lax.optimization_barrier((halves, early))
    swapped = lax.all_to_all(halves, "ao", 1, 2, tiled=True)
    occ_t = swapped[0]
    virt_t = swapped[1]
    v_part = jnp.einsum("mn,lnp->plm", virt_rows, occ_t, preferred_element_type=jnp.float32)
    w_part = jnp.einsum("kl,nlq->qnk", occ_rows, virt_t, preferred_element_type=jnp.float32)
    v_weights = weight_pair(v_part)
    w_weights = weight_pair(w_part)
    diag = slab_product(own_flat, w_weights)

    v_weights, w_weights, diag, late = lax.optimization_barrier(
        (v_weights, w_weights, diag, late)
    )
    received = [jnp.concatenate([a, b]) for a, b in zip(early, late)]
    total = jnp.zeros((rows, planes * rows), jnp.float32)
    total = add_cols(total, diag, plane)
    for slab, (route, recv_from, send_to) in zip(received, routes):
        source = jnp.array(recv_from, jnp.int32)[plane]
        target = jnp.array(send_to, jnp.int32)[plane]
        total = add_cols(total, slab_product(slab, v_weights).T, source)
        back = lax.ppermute(slab_product(slab, w_weights), "ri", [(d, s) for s, d in route])
        total = add_cols(total, back, target)

    width = total.shape[1] // cycle_size
    sent = total.reshape(rows, cycle_size, width).transpose(1, 0, 2)
    got = lax.all_to_all(sent, "ao", 0, 0, tiled=True)
    return jnp.sum(got, axis=0)


def solution(mesh):
    placed = (
        P("ri", "ao", None),
        P("ri", "ao", None),
        P("ao", None),
        P("ao", None),
        P("ao", None),
        P("ao", None),
        P("ao", None),
    )
    return jax.shard_map(
        per_device, mesh=mesh, in_specs=placed, out_specs=P("ri", "ao"), check_vma=False
    )
```

```python
import jax
import jax.numpy as jnp
from jax import lax
from jax.sharding import PartitionSpec as P

BS = 32
KS = 8
RB = 64


def screen_density(density, block_mask):
    own_blocks = block_mask.shape[0]
    all_blocks = block_mask.shape[1]
    shaped = density.reshape(own_blocks, BS, all_blocks, BS)
    keeper = block_mask.astype(density.dtype)[:, None, :, None]
    return (shaped * keeper).reshape(density.shape)


def pair_routes(size):
    routes = []
    for dist in range(1, size // 2 + 1):
        if 2 * dist < size:
            route = [(r, (r + dist) % size) for r in range(size)]
        else:
            route = []
            for i in range(size // 2):
                if i % 2 == 0:
                    route.append((i, i + dist))
                else:
                    route.append((i + dist, i))
        recv_from = list(range(size))
        send_to = list(range(size))
        for src, dst in route:
            recv_from[dst] = src
            send_to[src] = dst
        routes.append((route, recv_from, send_to))
    return routes


def mask_slab(slab, live):
    keeper = jnp.repeat(jnp.repeat(live[:, 0, :].astype(slab.dtype), RB, axis=0), BS, axis=1)
    return slab * keeper[:, None, :]


def split_hi_lo(values):
    rounded = lax.reduce_precision(values, exponent_bits=8, mantissa_bits=7)
    return rounded.astype(jnp.bfloat16), (values - rounded).astype(jnp.bfloat16)


def weight_pair(values):
    hi, lo = split_hi_lo(values)
    both = jnp.stack([hi, lo])
    return both.transpose(2, 3, 0, 1).reshape(values.shape[1] * values.shape[2], -1)


def slab_product(flat, weights):
    out = jnp.dot(flat, weights, preferred_element_type=jnp.float32)
    half = weights.shape[1] // 2
    return out[:, :half] + out[:, half:]


def add_cols(total, part, col_block):
    rows = part.shape[0]
    at = (jnp.int32(0), col_block * rows)
    here = lax.dynamic_slice(total, at, part.shape)
    return lax.dynamic_update_slice(total, here + part, at)


def per_device(tensor, live_blocks, occ_density, virt_density, occ_mask, virt_mask, pair_slots):
    rows = tensor.shape[0]
    assert tensor.shape[1] == BS
    planes = lax.axis_size("ri")
    cycle_size = lax.axis_size("ao")
    plane = lax.axis_index("ri")

    routes = pair_routes(planes)
    own = mask_slab(tensor, live_blocks)
    own_flat = own.reshape(rows, -1)
    lead = rows // 4
    early = [lax.ppermute(own_flat[:lead], "ri", route) for route, _, _ in routes]
    late = [lax.ppermute(own_flat[lead:], "ri", route) for route, _, _ in routes]

    stacked = jnp.stack(
        [screen_density(occ_density, occ_mask), screen_density(virt_density, virt_mask)]
    )
    full = lax.all_gather(stacked, "ao", axis=1, tiled=True)
    ao_total = full.shape[2]
    all_blocks = ao_total // BS
    picked = full.reshape(2, all_blocks, BS, ao_total)[:, pair_slots[0]]
    occ_rows = picked[0].reshape(KS * BS, ao_total)
    virt_rows = picked[1].reshape(KS * BS, ao_total)

    halves = jnp.einsum(
        "prk,dkc->dcrp",
        own,
        jnp.stack([occ_rows, virt_rows]),
        preferred_element_type=jnp.float32,
    ).astype(jnp.bfloat16)
    halves, early = lax.optimization_barrier((halves, early))
    swapped = lax.all_to_all(halves, "ao", 1, 2, tiled=True)
    occ_t = swapped[0]
    virt_t = swapped[1]
    v_part = jnp.einsum("mn,lnp->plm", virt_rows, occ_t, preferred_element_type=jnp.float32)
    w_part = jnp.einsum("kl,nlq->qnk", occ_rows, virt_t, preferred_element_type=jnp.float32)
    v_weights = weight_pair(v_part)
    w_weights = weight_pair(w_part)
    diag = slab_product(own_flat, w_weights)
    early_parts = [
        (slab_product(chunk, v_weights), slab_product(chunk, w_weights)) for chunk in early
    ]

    v_weights, w_weights, diag, early_parts, late = lax.optimization_barrier(
        (v_weights, w_weights, diag, early_parts, late)
    )
    total = jnp.zeros((rows, planes * rows), jnp.float32)
    total = add_cols(total, diag, plane)
    for (mine_e, theirs_e), chunk, (route, recv_from, send_to) in zip(early_parts, late, routes):
        source = jnp.array(recv_from, jnp.int32)[plane]
        target = jnp.array(send_to, jnp.int32)[plane]
        mine = jnp.concatenate([mine_e, slab_product(chunk, v_weights)])
        theirs = jnp.concatenate([theirs_e, slab_product(chunk, w_weights)])
        total = add_cols(total, mine.T, source)
        back = lax.ppermute(theirs, "ri", [(d, s) for s, d in route])
        total = add_cols(total, back, target)

    width = total.shape[1] // cycle_size
    sent = total.reshape(rows, cycle_size, width).transpose(1, 0, 2)
    got = lax.all_to_all(sent, "ao", 0, 0, tiled=True)
    return jnp.sum(got, axis=0)


def solution(mesh):
    placed = (
        P("ri", "ao", None),
        P("ri", "ao", None),
        P("ao", None),
        P("ao", None),
        P("ao", None),
        P("ao", None),
        P("ao", None),
    )
    return jax.shard_map(
        per_device, mesh=mesh, in_specs=placed, out_specs=P("ri", "ao"), check_vma=False
    )
```

```python
import jax
import jax.numpy as jnp
from jax import lax
from jax.sharding import PartitionSpec as P

BS = 32
KS = 8
RB = 64


def screen_density(density, block_mask):
    own_blocks = block_mask.shape[0]
    all_blocks = block_mask.shape[1]
    shaped = density.reshape(own_blocks, BS, all_blocks, BS)
    keeper = block_mask.astype(density.dtype)[:, None, :, None]
    return (shaped * keeper).reshape(density.shape)


def pair_routes(size):
    routes = []
    for dist in range(1, size // 2 + 1):
        if 2 * dist < size:
            route = [(r, (r + dist) % size) for r in range(size)]
        else:
            route = []
            for i in range(size // 2):
                if i % 2 == 0:
                    route.append((i, i + dist))
                else:
                    route.append((i + dist, i))
        recv_from = list(range(size))
        send_to = list(range(size))
        for src, dst in route:
            recv_from[dst] = src
            send_to[src] = dst
        routes.append((route, recv_from, send_to))
    return routes


def mask_slab(slab, live):
    keeper = jnp.repeat(jnp.repeat(live[:, 0, :].astype(slab.dtype), RB, axis=0), BS, axis=1)
    return slab * keeper[:, None, :]


def split_hi_lo(values):
    rounded = lax.reduce_precision(values, exponent_bits=8, mantissa_bits=7)
    return rounded.astype(jnp.bfloat16), (values - rounded).astype(jnp.bfloat16)


def weight_pair(values):
    hi, lo = split_hi_lo(values)
    both = jnp.stack([hi, lo])
    return both.transpose(2, 3, 0, 1).reshape(values.shape[1] * values.shape[2], -1)


def slab_product(flat, weights):
    out = jnp.dot(flat, weights, preferred_element_type=jnp.float32)
    half = weights.shape[1] // 2
    return out[:, :half] + out[:, half:]


def add_cols(total, part, col_block):
    rows = part.shape[0]
    at = (jnp.int32(0), col_block * rows)
    here = lax.dynamic_slice(total, at, part.shape)
    return lax.dynamic_update_slice(total, here + part, at)


def per_device(tensor, live_blocks, occ_density, virt_density, occ_mask, virt_mask, pair_slots):
    rows = tensor.shape[0]
    assert tensor.shape[1] == BS
    planes = lax.axis_size("ri")
    cycle_size = lax.axis_size("ao")
    plane = lax.axis_index("ri")

    routes = pair_routes(planes)
    own = mask_slab(tensor, live_blocks)
    own_flat = own.reshape(rows, -1)
    lead = rows // 4
    early = [lax.ppermute(own_flat[:lead], "ri", route) for route, _, _ in routes]
    late = [lax.ppermute(own_flat[lead:], "ri", route) for route, _, _ in routes]

    stacked = jnp.stack(
        [screen_density(occ_density, occ_mask), screen_density(virt_density, virt_mask)]
    )
    full = lax.all_gather(stacked, "ao", axis=1, tiled=True)
    ao_total = full.shape[2]
    all_blocks = ao_total // BS
    picked = full.reshape(2, all_blocks, BS, ao_total)[:, pair_slots[0]]
    occ_rows = picked[0].reshape(KS * BS, ao_total)
    virt_rows = picked[1].reshape(KS * BS, ao_total)

    halves = jnp.einsum(
        "prk,dkc->dcrp",
        own,
        jnp.stack([occ_rows, virt_rows]),
        preferred_element_type=jnp.float32,
    ).astype(jnp.bfloat16)
    halves, early = lax.optimization_barrier((halves, early))
    swapped = lax.all_to_all(halves, "ao", 1, 2, tiled=True)
    occ_t = swapped[0]
    virt_t = swapped[1]
    v_part = jnp.einsum("mn,lnp->plm", virt_rows, occ_t, preferred_element_type=jnp.float32)
    w_part = jnp.einsum("kl,nlq->qnk", occ_rows, virt_t, preferred_element_type=jnp.float32)
    v_weights = weight_pair(v_part)
    w_weights = weight_pair(w_part)
    diag = slab_product(own_flat, w_weights)

    v_weights, w_weights, diag, late = lax.optimization_barrier(
        (v_weights, w_weights, diag, late)
    )
    stacked_slabs = jnp.concatenate([part for pair in zip(early, late) for part in pair])
    mine_all = slab_product(stacked_slabs, v_weights)
    theirs_all = slab_product(stacked_slabs, w_weights)
    total = jnp.zeros((rows, planes * rows), jnp.float32)
    total = add_cols(total, diag, plane)
    for index, (route, recv_from, send_to) in enumerate(routes):
        source = jnp.array(recv_from, jnp.int32)[plane]
        target = jnp.array(send_to, jnp.int32)[plane]
        mine = mine_all[index * rows:(index + 1) * rows]
        theirs = theirs_all[index * rows:(index + 1) * rows]
        total = add_cols(total, mine.T, source)
        back = lax.ppermute(theirs, "ri", [(d, s) for s, d in route])
        total = add_cols(total, back, target)

    width = total.shape[1] // cycle_size
    sent = total.reshape(rows, cycle_size, width).transpose(1, 0, 2)
    got = lax.all_to_all(sent, "ao", 0, 0, tiled=True)
    return jnp.sum(got, axis=0)


def solution(mesh):
    placed = (
        P("ri", "ao", None),
        P("ri", "ao", None),
        P("ao", None),
        P("ao", None),
        P("ao", None),
        P("ao", None),
        P("ao", None),
    )
    return jax.shard_map(
        per_device, mesh=mesh, in_specs=placed, out_specs=P("ri", "ao"), check_vma=False
    )
```

```python
import jax
import jax.numpy as jnp
from jax import lax
from jax.sharding import PartitionSpec as P

BS = 32
KS = 8
RB = 64


def screen_density(density, block_mask):
    own_blocks = block_mask.shape[0]
    all_blocks = block_mask.shape[1]
    shaped = density.reshape(own_blocks, BS, all_blocks, BS)
    keeper = block_mask.astype(density.dtype)[:, None, :, None]
    return (shaped * keeper).reshape(density.shape)


def pair_routes(size):
    routes = []
    for dist in range(1, size // 2 + 1):
        if 2 * dist < size:
            route = [(r, (r + dist) % size) for r in range(size)]
        else:
            route = []
            for i in range(size // 2):
                if i % 2 == 0:
                    route.append((i, i + dist))
                else:
                    route.append((i + dist, i))
        recv_from = list(range(size))
        send_to = list(range(size))
        for src, dst in route:
            recv_from[dst] = src
            send_to[src] = dst
        routes.append((route, recv_from, send_to))
    return routes


def mask_slab(slab, live):
    keeper = jnp.repeat(jnp.repeat(live[:, 0, :].astype(slab.dtype), RB, axis=0), BS, axis=1)
    return slab * keeper[:, None, :]


def split_hi_lo(values):
    rounded = lax.reduce_precision(values, exponent_bits=8, mantissa_bits=7)
    return rounded.astype(jnp.bfloat16), (values - rounded).astype(jnp.bfloat16)


def weight_pair(values):
    hi, lo = split_hi_lo(values)
    both = jnp.stack([hi, lo])
    return both.transpose(2, 3, 0, 1).reshape(values.shape[1] * values.shape[2], -1)


def slab_product(flat, weights):
    out = jnp.dot(flat, weights, preferred_element_type=jnp.float32)
    half = weights.shape[1] // 2
    return out[:, :half] + out[:, half:]


def add_cols(total, part, col_block):
    rows = part.shape[0]
    at = (jnp.int32(0), col_block * rows)
    here = lax.dynamic_slice(total, at, part.shape)
    return lax.dynamic_update_slice(total, here + part, at)


def per_device(tensor, live_blocks, occ_density, virt_density, occ_mask, virt_mask, pair_slots):
    rows = tensor.shape[0]
    assert tensor.shape[1] == BS
    planes = lax.axis_size("ri")
    cycle_size = lax.axis_size("ao")
    plane = lax.axis_index("ri")

    routes = pair_routes(planes)
    own = mask_slab(tensor, live_blocks)
    own_flat = own.reshape(rows, -1)
    lead = rows // 4
    early = [lax.ppermute(own_flat[:lead], "ri", route) for route, _, _ in routes]
    late = [lax.ppermute(own_flat[lead:], "ri", route) for route, _, _ in routes]

    stacked = jnp.stack(
        [screen_density(occ_density, occ_mask), screen_density(virt_density, virt_mask)]
    )
    full = lax.all_gather(stacked, "ao", axis=1, tiled=True)
    ao_total = full.shape[2]
    all_blocks = ao_total // BS
    picked = full.reshape(2, all_blocks, BS, ao_total)[:, pair_slots[0]]
    occ_rows = picked[0].reshape(KS * BS, ao_total)
    virt_rows = picked[1].reshape(KS * BS, ao_total)

    halves = jnp.einsum(
        "prk,dkc->cdrp",
        own,
        jnp.stack([occ_rows, virt_rows]),
        preferred_element_type=jnp.float32,
    ).astype(jnp.bfloat16)
    halves, early = lax.optimization_barrier((halves, early))
    swapped = lax.all_to_all(halves, "ao", 0, 2, tiled=True)
    occ_t = swapped[:, 0]
    virt_t = swapped[:, 1]
    v_part = jnp.einsum("mn,lnp->plm", virt_rows, occ_t, preferred_element_type=jnp.float32)
    w_part = jnp.einsum("kl,nlq->qnk", occ_rows, virt_t, preferred_element_type=jnp.float32)
    v_weights = weight_pair(v_part)
    w_weights = weight_pair(w_part)
    diag = slab_product(own_flat, w_weights)

    v_weights, w_weights, diag, late = lax.optimization_barrier(
        (v_weights, w_weights, diag, late)
    )
    stacked_slabs = jnp.concatenate([part for pair in zip(early, late) for part in pair])
    mine_all = slab_product(stacked_slabs, v_weights)
    theirs_all = slab_product(stacked_slabs, w_weights)
    total = jnp.zeros((rows, planes * rows), jnp.float32)
    total = add_cols(total, diag, plane)
    for index, (route, recv_from, send_to) in enumerate(routes):
        source = jnp.array(recv_from, jnp.int32)[plane]
        target = jnp.array(send_to, jnp.int32)[plane]
        mine = mine_all[index * rows:(index + 1) * rows]
        theirs = theirs_all[index * rows:(index + 1) * rows]
        total = add_cols(total, mine.T, source)
        back = lax.ppermute(theirs, "ri", [(d, s) for s, d in route])
        total = add_cols(total, back, target)

    width = total.shape[1] // cycle_size
    sent = total.reshape(rows, cycle_size, width).transpose(1, 0, 2)
    got = lax.all_to_all(sent, "ao", 0, 0, tiled=True)
    return jnp.sum(got, axis=0)


def solution(mesh):
    placed = (
        P("ri", "ao", None),
        P("ri", "ao", None),
        P("ao", None),
        P("ao", None),
        P("ao", None),
        P("ao", None),
        P("ao", None),
    )
    return jax.shard_map(
        per_device, mesh=mesh, in_specs=placed, out_specs=P("ri", "ao"), check_vma=False
    )
```

```python
import jax
import jax.numpy as jnp
from jax import lax
from jax.sharding import PartitionSpec as P

BS = 32
KS = 8
RB = 64


def screen_density(density, block_mask):
    own_blocks = block_mask.shape[0]
    all_blocks = block_mask.shape[1]
    shaped = density.reshape(own_blocks, BS, all_blocks, BS)
    keeper = block_mask.astype(density.dtype)[:, None, :, None]
    return (shaped * keeper).reshape(density.shape)


def pair_routes(size):
    routes = []
    for dist in range(1, size // 2 + 1):
        if 2 * dist < size:
            route = [(r, (r + dist) % size) for r in range(size)]
        else:
            route = []
            for i in range(size // 2):
                if i % 2 == 0:
                    route.append((i, i + dist))
                else:
                    route.append((i + dist, i))
        recv_from = list(range(size))
        send_to = list(range(size))
        for src, dst in route:
            recv_from[dst] = src
            send_to[src] = dst
        routes.append((route, recv_from, send_to))
    return routes


def mask_slab(slab, live):
    keeper = jnp.repeat(jnp.repeat(live[:, 0, :].astype(slab.dtype), RB, axis=0), BS, axis=1)
    return slab * keeper[:, None, :]


def split_hi_lo(values):
    rounded = lax.reduce_precision(values, exponent_bits=8, mantissa_bits=7)
    return rounded.astype(jnp.bfloat16), (values - rounded).astype(jnp.bfloat16)


def weight_pair(values):
    hi, lo = split_hi_lo(values)
    both = jnp.stack([hi, lo])
    return both.transpose(2, 3, 0, 1).reshape(values.shape[1] * values.shape[2], -1)


def slab_product(flat, weights):
    out = jnp.dot(flat, weights, preferred_element_type=jnp.float32)
    half = weights.shape[1] // 2
    return out[:, :half] + out[:, half:]


def add_cols(total, part, col_block):
    rows = part.shape[0]
    at = (jnp.int32(0), col_block * rows)
    here = lax.dynamic_slice(total, at, part.shape)
    return lax.dynamic_update_slice(total, here + part, at)


def per_device(tensor, live_blocks, occ_density, virt_density, occ_mask, virt_mask, pair_slots):
    rows = tensor.shape[0]
    assert tensor.shape[1] == BS
    planes = lax.axis_size("ri")
    cycle_size = lax.axis_size("ao")
    plane = lax.axis_index("ri")

    routes = pair_routes(planes)
    own = mask_slab(tensor, live_blocks)
    own_flat = own.reshape(rows, -1)
    lead = rows // 4
    early = [lax.ppermute(own_flat[:lead], "ri", route) for route, _, _ in routes]
    late = [lax.ppermute(own_flat[lead:], "ri", route) for route, _, _ in routes]

    stacked = jnp.stack(
        [screen_density(occ_density, occ_mask), screen_density(virt_density, virt_mask)]
    )
    full = lax.all_gather(stacked, "ao", axis=1, tiled=True)
    ao_total = full.shape[2]
    all_blocks = ao_total // BS
    picked = full.reshape(2, all_blocks, BS, ao_total)[:, pair_slots[0]]
    occ_rows = picked[0].reshape(KS * BS, ao_total)
    virt_rows = picked[1].reshape(KS * BS, ao_total)

    halves = jnp.einsum(
        "prk,dkc->cdrp",
        own,
        jnp.stack([occ_rows, virt_rows]),
        preferred_element_type=jnp.float32,
    ).astype(jnp.bfloat16)
    halves, early = lax.optimization_barrier((halves, early))
    swapped = lax.all_to_all(halves, "ao", 0, 2, tiled=True)
    occ_t = swapped[:, 0]
    virt_t = swapped[:, 1]
    v_part = jnp.einsum("mn,lnp->plm", virt_rows, occ_t, preferred_element_type=jnp.float32)
    w_part = jnp.einsum("kl,nlq->qnk", occ_rows, virt_t, preferred_element_type=jnp.float32)
    v_weights = weight_pair(v_part)
    w_weights = weight_pair(w_part)
    diag = slab_product(own_flat, w_weights)
    early_stack = jnp.concatenate(early)
    early_mine = slab_product(early_stack, v_weights)
    early_theirs = slab_product(early_stack, w_weights)

    v_weights, w_weights, diag, early_mine, early_theirs, late = lax.optimization_barrier(
        (v_weights, w_weights, diag, early_mine, early_theirs, late)
    )
    late_stack = jnp.concatenate(late)
    late_mine = slab_product(late_stack, v_weights)
    late_theirs = slab_product(late_stack, w_weights)
    count = len(routes)
    lead = rows // 4
    rest = rows - lead

    def slab_rows(early_part, late_part, index):
        return jnp.concatenate(
            [early_part[index * lead:(index + 1) * lead], late_part[index * rest:(index + 1) * rest]]
        )

    mine_all = jnp.concatenate([slab_rows(early_mine, late_mine, i) for i in range(count)])
    theirs_all = jnp.concatenate([slab_rows(early_theirs, late_theirs, i) for i in range(count)])
    total = jnp.zeros((rows, planes * rows), jnp.float32)
    total = add_cols(total, diag, plane)
    for index, (route, recv_from, send_to) in enumerate(routes):
        source = jnp.array(recv_from, jnp.int32)[plane]
        target = jnp.array(send_to, jnp.int32)[plane]
        mine = mine_all[index * rows:(index + 1) * rows]
        theirs = theirs_all[index * rows:(index + 1) * rows]
        total = add_cols(total, mine.T, source)
        back = lax.ppermute(theirs, "ri", [(d, s) for s, d in route])
        total = add_cols(total, back, target)

    width = total.shape[1] // cycle_size
    sent = total.reshape(rows, cycle_size, width).transpose(1, 0, 2)
    got = lax.all_to_all(sent, "ao", 0, 0, tiled=True)
    return jnp.sum(got, axis=0)


def solution(mesh):
    placed = (
        P("ri", "ao", None),
        P("ri", "ao", None),
        P("ao", None),
        P("ao", None),
        P("ao", None),
        P("ao", None),
        P("ao", None),
    )
    return jax.shard_map(
        per_device, mesh=mesh, in_specs=placed, out_specs=P("ri", "ao"), check_vma=False
    )
```

```python
import jax
import jax.numpy as jnp
from jax import lax
from jax.sharding import PartitionSpec as P

BS = 32
KS = 8
RB = 64


def screen_density(density, block_mask):
    own_blocks = block_mask.shape[0]
    all_blocks = block_mask.shape[1]
    shaped = density.reshape(own_blocks, BS, all_blocks, BS)
    keeper = block_mask.astype(density.dtype)[:, None, :, None]
    return (shaped * keeper).reshape(density.shape)


def pair_routes(size):
    routes = []
    for dist in range(1, size // 2 + 1):
        if 2 * dist < size:
            route = [(r, (r + dist) % size) for r in range(size)]
        else:
            route = []
            for i in range(size // 2):
                if i % 2 == 0:
                    route.append((i, i + dist))
                else:
                    route.append((i + dist, i))
        recv_from = list(range(size))
        send_to = list(range(size))
        for src, dst in route:
            recv_from[dst] = src
            send_to[src] = dst
        routes.append((route, recv_from, send_to))
    return routes


def mask_slab(slab, live):
    keeper = jnp.repeat(jnp.repeat(live[:, 0, :].astype(slab.dtype), RB, axis=0), BS, axis=1)
    return slab * keeper[:, None, :]


def split_hi_lo(values):
    rounded = lax.reduce_precision(values, exponent_bits=8, mantissa_bits=7)
    return rounded.astype(jnp.bfloat16), (values - rounded).astype(jnp.bfloat16)


def weight_pair(values):
    hi, lo = split_hi_lo(values)
    both = jnp.stack([hi, lo])
    return both.transpose(2, 3, 0, 1).reshape(values.shape[1] * values.shape[2], -1)


def slab_product(flat, weights):
    out = jnp.dot(flat, weights, preferred_element_type=jnp.float32)
    half = weights.shape[1] // 2
    return out[:, :half] + out[:, half:]


def add_cols(total, part, col_block):
    rows = part.shape[0]
    at = (jnp.int32(0), col_block * rows)
    here = lax.dynamic_slice(total, at, part.shape)
    return lax.dynamic_update_slice(total, here + part, at)


def per_device(tensor, live_blocks, occ_density, virt_density, occ_mask, virt_mask, pair_slots):
    rows = tensor.shape[0]
    assert tensor.shape[1] == BS
    planes = lax.axis_size("ri")
    cycle_size = lax.axis_size("ao")
    plane = lax.axis_index("ri")

    routes = pair_routes(planes)
    own = mask_slab(tensor, live_blocks)
    own_flat = own.reshape(rows, -1)
    lead = rows // 4
    early = [lax.ppermute(own_flat[:lead], "ri", route) for route, _, _ in routes]
    late = [lax.ppermute(own_flat[lead:], "ri", route) for route, _, _ in routes]

    stacked = jnp.stack(
        [screen_density(occ_density, occ_mask), screen_density(virt_density, virt_mask)]
    )
    full = lax.all_gather(stacked, "ao", axis=1, tiled=True)
    ao_total = full.shape[2]
    all_blocks = ao_total // BS
    picked = full.reshape(2, all_blocks, BS, ao_total)[:, pair_slots[0]]
    occ_rows = picked[0].reshape(KS * BS, ao_total)
    virt_rows = picked[1].reshape(KS * BS, ao_total)

    halves = jnp.einsum(
        "prk,dkc->cdrp",
        own,
        jnp.stack([occ_rows, virt_rows]),
        preferred_element_type=jnp.float32,
    ).astype(jnp.bfloat16)
    halves, early = lax.optimization_barrier((halves, early))
    swapped = lax.all_to_all(halves, "ao", 0, 2, tiled=True)
    occ_t = swapped[:, 0]
    virt_t = swapped[:, 1]
    v_part = jnp.einsum("mn,lnp->plm", virt_rows, occ_t, preferred_element_type=jnp.float32)
    w_part = jnp.einsum("kl,nlq->qnk", occ_rows, virt_t, preferred_element_type=jnp.float32)
    v_weights = weight_pair(v_part)
    w_weights = weight_pair(w_part)
    early_stack = jnp.concatenate(early)
    early_mine = slab_product(early_stack, v_weights)
    with_own = slab_product(jnp.concatenate([own_flat, early_stack]), w_weights)
    diag = with_own[:rows]
    early_theirs = with_own[rows:]

    v_weights, w_weights, diag, early_mine, early_theirs, late = lax.optimization_barrier(
        (v_weights, w_weights, diag, early_mine, early_theirs, late)
    )
    late_stack = jnp.concatenate(late)
    late_mine = slab_product(late_stack, v_weights)
    late_theirs = slab_product(late_stack, w_weights)
    count = len(routes)
    lead = rows // 4
    rest = rows - lead

    def slab_rows(early_part, late_part, index):
        return jnp.concatenate(
            [early_part[index * lead:(index + 1) * lead], late_part[index * rest:(index + 1) * rest]]
        )

    mine_all = jnp.concatenate([slab_rows(early_mine, late_mine, i) for i in range(count)])
    theirs_all = jnp.concatenate([slab_rows(early_theirs, late_theirs, i) for i in range(count)])
    total = jnp.zeros((rows, planes * rows), jnp.float32)
    total = add_cols(total, diag, plane)
    for index, (route, recv_from, send_to) in enumerate(routes):
        source = jnp.array(recv_from, jnp.int32)[plane]
        target = jnp.array(send_to, jnp.int32)[plane]
        mine = mine_all[index * rows:(index + 1) * rows]
        theirs = theirs_all[index * rows:(index + 1) * rows]
        total = add_cols(total, mine.T, source)
        back = lax.ppermute(theirs, "ri", [(d, s) for s, d in route])
        total = add_cols(total, back, target)

    width = total.shape[1] // cycle_size
    sent = total.reshape(rows, cycle_size, width).transpose(1, 0, 2)
    got = lax.all_to_all(sent, "ao", 0, 0, tiled=True)
    return jnp.sum(got, axis=0)


def solution(mesh):
    placed = (
        P("ri", "ao", None),
        P("ri", "ao", None),
        P("ao", None),
        P("ao", None),
        P("ao", None),
        P("ao", None),
        P("ao", None),
    )
    return jax.shard_map(
        per_device, mesh=mesh, in_specs=placed, out_specs=P("ri", "ao"), check_vma=False
    )
```

```python
import jax
import jax.numpy as jnp
from jax import lax
from jax.sharding import PartitionSpec as P

BS = 32
KS = 8
RB = 64


def screen_density(density, block_mask):
    own_blocks = block_mask.shape[0]
    all_blocks = block_mask.shape[1]
    shaped = density.reshape(own_blocks, BS, all_blocks, BS)
    keeper = block_mask.astype(density.dtype)[:, None, :, None]
    return (shaped * keeper).reshape(density.shape)


def pair_routes(size):
    routes = []
    for dist in range(1, size // 2 + 1):
        if 2 * dist < size:
            route = [(r, (r + dist) % size) for r in range(size)]
        else:
            route = []
            for i in range(size // 2):
                if i % 2 == 0:
                    route.append((i, i + dist))
                else:
                    route.append((i + dist, i))
        recv_from = list(range(size))
        send_to = list(range(size))
        for src, dst in route:
            recv_from[dst] = src
            send_to[src] = dst
        routes.append((route, recv_from, send_to))
    return routes


def mask_slab(slab, live):
    keeper = jnp.repeat(jnp.repeat(live[:, 0, :].astype(slab.dtype), RB, axis=0), BS, axis=1)
    return slab * keeper[:, None, :]


def split_hi_lo(values):
    rounded = lax.reduce_precision(values, exponent_bits=8, mantissa_bits=7)
    return rounded.astype(jnp.bfloat16), (values - rounded).astype(jnp.bfloat16)


def weight_pair(values):
    hi, lo = split_hi_lo(values)
    groups = 2
    width = values.shape[0] // groups
    both = jnp.stack([hi, lo]).reshape(2, groups, width, values.shape[1], values.shape[2])
    both = both.transpose(3, 4, 1, 0, 2)
    return both.reshape(values.shape[1] * values.shape[2], -1)


def slab_product(flat, weights):
    out = jnp.dot(flat, weights, preferred_element_type=jnp.float32)
    width = weights.shape[1] // 4
    parts = out.reshape(out.shape[0], 2, 2, width)
    return (parts[:, :, 0] + parts[:, :, 1]).reshape(out.shape[0], 2 * width)


def add_cols(total, part, col_block):
    rows = part.shape[0]
    at = (jnp.int32(0), col_block * rows)
    here = lax.dynamic_slice(total, at, part.shape)
    return lax.dynamic_update_slice(total, here + part, at)


def per_device(tensor, live_blocks, occ_density, virt_density, occ_mask, virt_mask, pair_slots):
    rows = tensor.shape[0]
    assert tensor.shape[1] == BS
    planes = lax.axis_size("ri")
    cycle_size = lax.axis_size("ao")
    plane = lax.axis_index("ri")

    routes = pair_routes(planes)
    own = mask_slab(tensor, live_blocks)
    own_flat = own.reshape(rows, -1)
    lead = rows // 4
    early = [lax.ppermute(own_flat[:lead], "ri", route) for route, _, _ in routes]
    late = [lax.ppermute(own_flat[lead:], "ri", route) for route, _, _ in routes]

    stacked = jnp.stack(
        [screen_density(occ_density, occ_mask), screen_density(virt_density, virt_mask)]
    )
    full = lax.all_gather(stacked, "ao", axis=1, tiled=True)
    ao_total = full.shape[2]
    all_blocks = ao_total // BS
    picked = full.reshape(2, all_blocks, BS, ao_total)[:, pair_slots[0]]
    occ_rows = picked[0].reshape(KS * BS, ao_total)
    virt_rows = picked[1].reshape(KS * BS, ao_total)

    halves = jnp.einsum(
        "prk,dkc->cdrp",
        own,
        jnp.stack([occ_rows, virt_rows]),
        preferred_element_type=jnp.float32,
    ).astype(jnp.bfloat16)
    halves, early = lax.optimization_barrier((halves, early))
    swapped = lax.all_to_all(halves, "ao", 0, 2, tiled=True)
    occ_t = swapped[:, 0]
    virt_t = swapped[:, 1]
    v_part = jnp.einsum("mn,lnp->plm", virt_rows, occ_t, preferred_element_type=jnp.float32)
    w_part = jnp.einsum("kl,nlq->qnk", occ_rows, virt_t, preferred_element_type=jnp.float32)
    weights = weight_pair(jnp.concatenate([v_part, w_part]))
    early_stack = jnp.concatenate(early)
    with_own = slab_product(jnp.concatenate([own_flat, early_stack]), weights)
    diag = with_own[:rows, rows:]
    early_mine = with_own[rows:, :rows]
    early_theirs = with_own[rows:, rows:]

    weights, diag, early_mine, early_theirs, late = lax.optimization_barrier(
        (weights, diag, early_mine, early_theirs, late)
    )
    late_stack = jnp.concatenate(late)
    late_both = slab_product(late_stack, weights)
    late_mine = late_both[:, :rows]
    late_theirs = late_both[:, rows:]
    count = len(routes)
    lead = rows // 4
    rest = rows - lead

    def slab_rows(early_part, late_part, index):
        return jnp.concatenate(
            [early_part[index * lead:(index + 1) * lead], late_part[index * rest:(index + 1) * rest]]
        )

    mine_all = jnp.concatenate([slab_rows(early_mine, late_mine, i) for i in range(count)])
    theirs_all = jnp.concatenate([slab_rows(early_theirs, late_theirs, i) for i in range(count)])
    total = jnp.zeros((rows, planes * rows), jnp.float32)
    total = add_cols(total, diag, plane)
    for index, (route, recv_from, send_to) in enumerate(routes):
        source = jnp.array(recv_from, jnp.int32)[plane]
        target = jnp.array(send_to, jnp.int32)[plane]
        mine = mine_all[index * rows:(index + 1) * rows]
        theirs = theirs_all[index * rows:(index + 1) * rows]
        total = add_cols(total, mine.T, source)
        back = lax.ppermute(theirs, "ri", [(d, s) for s, d in route])
        total = add_cols(total, back, target)

    width = total.shape[1] // cycle_size
    sent = total.reshape(rows, cycle_size, width).transpose(1, 0, 2)
    got = lax.all_to_all(sent, "ao", 0, 0, tiled=True)
    return jnp.sum(got, axis=0)


def solution(mesh):
    placed = (
        P("ri", "ao", None),
        P("ri", "ao", None),
        P("ao", None),
        P("ao", None),
        P("ao", None),
        P("ao", None),
        P("ao", None),
    )
    return jax.shard_map(
        per_device, mesh=mesh, in_specs=placed, out_specs=P("ri", "ao"), check_vma=False
    )
```

```python
import jax
import jax.numpy as jnp
from jax import lax
from jax.sharding import PartitionSpec as P

BS = 32
KS = 8
RB = 64


def screen_density(density, block_mask):
    own_blocks = block_mask.shape[0]
    all_blocks = block_mask.shape[1]
    shaped = density.reshape(own_blocks, BS, all_blocks, BS)
    keeper = block_mask.astype(density.dtype)[:, None, :, None]
    return (shaped * keeper).reshape(density.shape)


def pair_routes(size):
    routes = []
    for dist in range(1, size // 2 + 1):
        if 2 * dist < size:
            route = [(r, (r + dist) % size) for r in range(size)]
        else:
            route = []
            for i in range(size // 2):
                if i % 2 == 0:
                    route.append((i, i + dist))
                else:
                    route.append((i + dist, i))
        recv_from = list(range(size))
        send_to = list(range(size))
        for src, dst in route:
            recv_from[dst] = src
            send_to[src] = dst
        routes.append((route, recv_from, send_to))
    return routes


def mask_slab(slab, live):
    keeper = jnp.repeat(jnp.repeat(live[:, 0, :].astype(slab.dtype), RB, axis=0), BS, axis=1)
    return slab * keeper[:, None, :]


def split_hi_lo(values):
    rounded = lax.reduce_precision(values, exponent_bits=8, mantissa_bits=7)
    return rounded.astype(jnp.bfloat16), (values - rounded).astype(jnp.bfloat16)


def weight_pair(values):
    hi, lo = split_hi_lo(values)
    both = jnp.stack([hi, lo])
    return both.transpose(2, 3, 0, 1).reshape(values.shape[1] * values.shape[2], -1)


def slab_product(flat, weights):
    out = jnp.dot(flat, weights, preferred_element_type=jnp.float32)
    half = weights.shape[1] // 2
    return out[:, :half] + out[:, half:]


def add_cols(total, part, col_block):
    rows = part.shape[0]
    at = (jnp.int32(0), col_block * rows)
    here = lax.dynamic_slice(total, at, part.shape)
    return lax.dynamic_update_slice(total, here + part, at)


def per_device(tensor, live_blocks, occ_density, virt_density, occ_mask, virt_mask, pair_slots):
    rows = tensor.shape[0]
    assert tensor.shape[1] == BS
    planes = lax.axis_size("ri")
    cycle_size = lax.axis_size("ao")
    plane = lax.axis_index("ri")

    routes = pair_routes(planes)
    own = mask_slab(tensor, live_blocks)
    own_flat = own.reshape(rows, -1)
    lead = rows // 4
    early = [lax.ppermute(own_flat[:lead], "ri", route) for route, _, _ in routes]
    late_source = own_flat[lead:]

    stacked = jnp.stack(
        [screen_density(occ_density, occ_mask), screen_density(virt_density, virt_mask)]
    )
    full = lax.all_gather(stacked, "ao", axis=1, tiled=True)
    ao_total = full.shape[2]
    all_blocks = ao_total // BS
    picked = full.reshape(2, all_blocks, BS, ao_total)[:, pair_slots[0]]
    occ_rows = picked[0].reshape(KS * BS, ao_total)
    virt_rows = picked[1].reshape(KS * BS, ao_total)

    halves = jnp.einsum(
        "prk,dkc->cdrp",
        own,
        jnp.stack([occ_rows, virt_rows]),
        preferred_element_type=jnp.float32,
    ).astype(jnp.bfloat16)
    halves, early, late_source = lax.optimization_barrier((halves, early, late_source))
    late = [lax.ppermute(late_source, "ri", route) for route, _, _ in routes]
    swapped = lax.all_to_all(halves, "ao", 0, 2, tiled=True)
    occ_t = swapped[:, 0]
    virt_t = swapped[:, 1]
    v_part = jnp.einsum("mn,lnp->plm", virt_rows, occ_t, preferred_element_type=jnp.float32)
    w_part = jnp.einsum("kl,nlq->qnk", occ_rows, virt_t, preferred_element_type=jnp.float32)
    v_weights = weight_pair(v_part)
    w_weights = weight_pair(w_part)
    early_stack = jnp.concatenate(early)
    early_mine = slab_product(early_stack, v_weights)
    with_own = slab_product(jnp.concatenate([own_flat, early_stack]), w_weights)
    diag = with_own[:rows]
    early_theirs = with_own[rows:]

    v_weights, w_weights, diag, early_mine, early_theirs, late = lax.optimization_barrier(
        (v_weights, w_weights, diag, early_mine, early_theirs, late)
    )
    late_stack = jnp.concatenate(late)
    late_mine = slab_product(late_stack, v_weights)
    late_theirs = slab_product(late_stack, w_weights)
    count = len(routes)
    lead = rows // 4
    rest = rows - lead

    def slab_rows(early_part, late_part, index):
        return jnp.concatenate(
            [early_part[index * lead:(index + 1) * lead], late_part[index * rest:(index + 1) * rest]]
        )

    mine_all = jnp.concatenate([slab_rows(early_mine, late_mine, i) for i in range(count)])
    theirs_all = jnp.concatenate([slab_rows(early_theirs, late_theirs, i) for i in range(count)])
    total = jnp.zeros((rows, planes * rows), jnp.float32)
    total = add_cols(total, diag, plane)
    for index, (route, recv_from, send_to) in enumerate(routes):
        source = jnp.array(recv_from, jnp.int32)[plane]
        target = jnp.array(send_to, jnp.int32)[plane]
        mine = mine_all[index * rows:(index + 1) * rows]
        theirs = theirs_all[index * rows:(index + 1) * rows]
        total = add_cols(total, mine.T, source)
        back = lax.ppermute(theirs, "ri", [(d, s) for s, d in route])
        total = add_cols(total, back, target)

    width = total.shape[1] // cycle_size
    sent = total.reshape(rows, cycle_size, width).transpose(1, 0, 2)
    got = lax.all_to_all(sent, "ao", 0, 0, tiled=True)
    return jnp.sum(got, axis=0)


def solution(mesh):
    placed = (
        P("ri", "ao", None),
        P("ri", "ao", None),
        P("ao", None),
        P("ao", None),
        P("ao", None),
        P("ao", None),
        P("ao", None),
    )
    return jax.shard_map(
        per_device, mesh=mesh, in_specs=placed, out_specs=P("ri", "ao"), check_vma=False
    )
```

```python
import jax
import jax.numpy as jnp
from jax import lax
from jax.sharding import PartitionSpec as P

BS = 32
KS = 8
RB = 64


def screen_density(density, block_mask):
    own_blocks = block_mask.shape[0]
    all_blocks = block_mask.shape[1]
    shaped = density.reshape(own_blocks, BS, all_blocks, BS)
    keeper = block_mask.astype(density.dtype)[:, None, :, None]
    return (shaped * keeper).reshape(density.shape)


def pair_routes(size):
    routes = []
    for dist in range(1, size // 2 + 1):
        if 2 * dist < size:
            route = [(r, (r + dist) % size) for r in range(size)]
        else:
            route = []
            for i in range(size // 2):
                if i % 2 == 0:
                    route.append((i, i + dist))
                else:
                    route.append((i + dist, i))
        recv_from = list(range(size))
        send_to = list(range(size))
        for src, dst in route:
            recv_from[dst] = src
            send_to[src] = dst
        routes.append((route, recv_from, send_to))
    return routes


def mask_slab(slab, live):
    keeper = jnp.repeat(jnp.repeat(live[:, 0, :].astype(slab.dtype), RB, axis=0), BS, axis=1)
    return slab * keeper[:, None, :]


def split_hi_lo(values):
    rounded = lax.reduce_precision(values, exponent_bits=8, mantissa_bits=7)
    return rounded.astype(jnp.bfloat16), (values - rounded).astype(jnp.bfloat16)


def weight_pair(values):
    hi, lo = split_hi_lo(values)
    both = jnp.stack([hi, lo])
    return both.transpose(2, 3, 0, 1).reshape(values.shape[1] * values.shape[2], -1)


def slab_product(flat, weights):
    out = jnp.dot(flat, weights, preferred_element_type=jnp.float32)
    half = weights.shape[1] // 2
    return out[:, :half] + out[:, half:]


def add_cols(total, part, col_block):
    rows = part.shape[0]
    at = (jnp.int32(0), col_block * rows)
    here = lax.dynamic_slice(total, at, part.shape)
    return lax.dynamic_update_slice(total, here + part, at)


def per_device(tensor, live_blocks, occ_density, virt_density, occ_mask, virt_mask, pair_slots):
    rows = tensor.shape[0]
    assert tensor.shape[1] == BS
    planes = lax.axis_size("ri")
    cycle_size = lax.axis_size("ao")
    plane = lax.axis_index("ri")

    routes = pair_routes(planes)
    own = mask_slab(tensor, live_blocks)
    own_flat = own.reshape(rows, -1)
    lead = rows // 4
    early = [lax.ppermute(own_flat[:lead], "ri", route) for route, _, _ in routes]
    late = [lax.ppermute(own_flat[lead:], "ri", route) for route, _, _ in routes]

    stacked = jnp.stack(
        [screen_density(occ_density, occ_mask), screen_density(virt_density, virt_mask)]
    )
    full = lax.all_gather(stacked, "ao", axis=1, tiled=True)
    ao_total = full.shape[2]
    all_blocks = ao_total // BS
    picked = full.reshape(2, all_blocks, BS, ao_total)[:, pair_slots[0]]
    occ_rows = picked[0].reshape(KS * BS, ao_total)
    virt_rows = picked[1].reshape(KS * BS, ao_total)

    halves = jnp.einsum(
        "prk,dkc->cdrp",
        own,
        jnp.stack([occ_rows, virt_rows]),
        preferred_element_type=jnp.float32,
    ).astype(jnp.bfloat16)
    halves, early = lax.optimization_barrier((halves, early))
    swapped = lax.all_to_all(halves, "ao", 0, 2, tiled=True)
    occ_t = swapped[:, 0]
    virt_t = swapped[:, 1]
    v_part = jnp.einsum("mn,lnp->plm", virt_rows, occ_t, preferred_element_type=jnp.float32)
    w_part = jnp.einsum("kl,nlq->qnk", occ_rows, virt_t, preferred_element_type=jnp.float32)
    v_weights = weight_pair(v_part)
    w_weights = weight_pair(w_part)
    early_stack = jnp.concatenate(early)
    early_mine = slab_product(early_stack, v_weights)
    with_own = slab_product(jnp.concatenate([own_flat, early_stack]), w_weights)
    diag = with_own[:rows]
    early_theirs = with_own[rows:]

    v_weights, w_weights, diag, early_mine, early_theirs, late = lax.optimization_barrier(
        (v_weights, w_weights, diag, early_mine, early_theirs, late)
    )
    late_stack = jnp.concatenate(late)
    late_mine = slab_product(late_stack, v_weights)
    late_theirs = slab_product(late_stack, w_weights)
    count = len(routes)
    lead = rows // 4
    rest = rows - lead

    def slab_rows(early_part, late_part, index):
        return jnp.concatenate(
            [early_part[index * lead:(index + 1) * lead], late_part[index * rest:(index + 1) * rest]]
        )

    mine_all = jnp.concatenate([slab_rows(early_mine, late_mine, i) for i in range(count)])
    theirs_all = jnp.concatenate([slab_rows(early_theirs, late_theirs, i) for i in range(count)])
    total = jnp.zeros((rows, planes * rows), jnp.float32)
    total = add_cols(total, diag, plane)
    total_t = jnp.zeros((planes * rows, rows), jnp.float32)
    for index, (route, recv_from, send_to) in enumerate(routes):
        source = jnp.array(recv_from, jnp.int32)[plane]
        target = jnp.array(send_to, jnp.int32)[plane]
        mine = mine_all[index * rows:(index + 1) * rows]
        theirs = theirs_all[index * rows:(index + 1) * rows]
        at = (source * rows, jnp.int32(0))
        here = lax.dynamic_slice(total_t, at, mine.shape)
        total_t = lax.dynamic_update_slice(total_t, here + mine, at)
        back = lax.ppermute(theirs, "ri", [(d, s) for s, d in route])
        total = add_cols(total, back, target)
    total = total + total_t.T

    width = total.shape[1] // cycle_size
    sent = total.reshape(rows, cycle_size, width).transpose(1, 0, 2)
    got = lax.all_to_all(sent, "ao", 0, 0, tiled=True)
    return jnp.sum(got, axis=0)


def solution(mesh):
    placed = (
        P("ri", "ao", None),
        P("ri", "ao", None),
        P("ao", None),
        P("ao", None),
        P("ao", None),
        P("ao", None),
        P("ao", None),
    )
    return jax.shard_map(
        per_device, mesh=mesh, in_specs=placed, out_specs=P("ri", "ao"), check_vma=False
    )
```

```python
import jax
import jax.numpy as jnp
from jax import lax
from jax.experimental.layout import Layout, with_layout_constraint
from jax.sharding import PartitionSpec as P

BS = 32
KS = 8
RB = 64


def screen_density(density, block_mask):
    own_blocks = block_mask.shape[0]
    all_blocks = block_mask.shape[1]
    shaped = density.reshape(own_blocks, BS, all_blocks, BS)
    keeper = block_mask.astype(density.dtype)[:, None, :, None]
    return (shaped * keeper).reshape(density.shape)


def pair_routes(size):
    routes = []
    for dist in range(1, size // 2 + 1):
        if 2 * dist < size:
            route = [(r, (r + dist) % size) for r in range(size)]
        else:
            route = []
            for i in range(size // 2):
                if i % 2 == 0:
                    route.append((i, i + dist))
                else:
                    route.append((i + dist, i))
        recv_from = list(range(size))
        send_to = list(range(size))
        for src, dst in route:
            recv_from[dst] = src
            send_to[src] = dst
        routes.append((route, recv_from, send_to))
    return routes


def mask_slab(slab, live):
    keeper = jnp.repeat(jnp.repeat(live[:, 0, :].astype(slab.dtype), RB, axis=0), BS, axis=1)
    return slab * keeper[:, None, :]


def split_hi_lo(values):
    rounded = lax.reduce_precision(values, exponent_bits=8, mantissa_bits=7)
    return rounded.astype(jnp.bfloat16), (values - rounded).astype(jnp.bfloat16)


def weight_pair(values):
    hi, lo = split_hi_lo(values)
    both = jnp.stack([hi, lo])
    return both.transpose(2, 3, 0, 1).reshape(values.shape[1] * values.shape[2], -1)


def slab_product(flat, weights):
    out = jnp.dot(flat, weights, preferred_element_type=jnp.float32)
    half = weights.shape[1] // 2
    return out[:, :half] + out[:, half:]


def add_cols(total, part, col_block):
    rows = part.shape[0]
    at = (jnp.int32(0), col_block * rows)
    here = lax.dynamic_slice(total, at, part.shape)
    return lax.dynamic_update_slice(total, here + part, at)


def per_device(tensor, live_blocks, occ_density, virt_density, occ_mask, virt_mask, pair_slots):
    rows = tensor.shape[0]
    assert tensor.shape[1] == BS
    planes = lax.axis_size("ri")
    cycle_size = lax.axis_size("ao")
    plane = lax.axis_index("ri")

    routes = pair_routes(planes)
    own = mask_slab(tensor, live_blocks)
    own_flat = own.reshape(rows, -1)
    lead = rows // 4
    early = [lax.ppermute(own_flat[:lead], "ri", route) for route, _, _ in routes]
    late = [lax.ppermute(own_flat[lead:], "ri", route) for route, _, _ in routes]

    stacked = jnp.stack(
        [screen_density(occ_density, occ_mask), screen_density(virt_density, virt_mask)]
    )
    full = lax.all_gather(stacked, "ao", axis=1, tiled=True)
    ao_total = full.shape[2]
    all_blocks = ao_total // BS
    picked = full.reshape(2, all_blocks, BS, ao_total)[:, pair_slots[0]]
    occ_rows = picked[0].reshape(KS * BS, ao_total)
    virt_rows = picked[1].reshape(KS * BS, ao_total)

    halves = jnp.einsum(
        "prk,dkc->cdrp",
        own,
        jnp.stack([occ_rows, virt_rows]),
        preferred_element_type=jnp.float32,
    ).astype(jnp.bfloat16)
    halves = with_layout_constraint(halves, Layout(major_to_minor=(0, 1, 2, 3)))
    halves, early = lax.optimization_barrier((halves, early))
    swapped = lax.all_to_all(halves, "ao", 0, 2, tiled=True)
    occ_t = swapped[:, 0]
    virt_t = swapped[:, 1]
    v_part = jnp.einsum("mn,lnp->plm", virt_rows, occ_t, preferred_element_type=jnp.float32)
    w_part = jnp.einsum("kl,nlq->qnk", occ_rows, virt_t, preferred_element_type=jnp.float32)
    v_weights = weight_pair(v_part)
    w_weights = weight_pair(w_part)
    early_stack = jnp.concatenate(early)
    early_mine = slab_product(early_stack, v_weights)
    with_own = slab_product(jnp.concatenate([own_flat, early_stack]), w_weights)
    diag = with_own[:rows]
    early_theirs = with_own[rows:]

    v_weights, w_weights, diag, early_mine, early_theirs, late = lax.optimization_barrier(
        (v_weights, w_weights, diag, early_mine, early_theirs, late)
    )
    late_stack = jnp.concatenate(late)
    late_mine = slab_product(late_stack, v_weights)
    late_theirs = slab_product(late_stack, w_weights)
    count = len(routes)
    lead = rows // 4
    rest = rows - lead

    def slab_rows(early_part, late_part, index):
        return jnp.concatenate(
            [early_part[index * lead:(index + 1) * lead], late_part[index * rest:(index + 1) * rest]]
        )

    mine_all = jnp.concatenate([slab_rows(early_mine, late_mine, i) for i in range(count)])
    theirs_all = jnp.concatenate([slab_rows(early_theirs, late_theirs, i) for i in range(count)])
    total = jnp.zeros((rows, planes * rows), jnp.float32)
    total = add_cols(total, diag, plane)
    for index, (route, recv_from, send_to) in enumerate(routes):
        source = jnp.array(recv_from, jnp.int32)[plane]
        target = jnp.array(send_to, jnp.int32)[plane]
        mine = mine_all[index * rows:(index + 1) * rows]
        theirs = theirs_all[index * rows:(index + 1) * rows]
        total = add_cols(total, mine.T, source)
        back = lax.ppermute(theirs, "ri", [(d, s) for s, d in route])
        total = add_cols(total, back, target)

    width = total.shape[1] // cycle_size
    sent = total.reshape(rows, cycle_size, width).transpose(1, 0, 2)
    got = lax.all_to_all(sent, "ao", 0, 0, tiled=True)
    return jnp.sum(got, axis=0)


def solution(mesh):
    placed = (
        P("ri", "ao", None),
        P("ri", "ao", None),
        P("ao", None),
        P("ao", None),
        P("ao", None),
        P("ao", None),
        P("ao", None),
    )
    return jax.shard_map(
        per_device, mesh=mesh, in_specs=placed, out_specs=P("ri", "ao"), check_vma=False
    )
```

```python
import jax
import jax.numpy as jnp
from jax import lax
from jax.experimental.layout import Layout, with_layout_constraint
from jax.sharding import PartitionSpec as P

BS = 32
KS = 8
RB = 64


def screen_density(density, block_mask):
    own_blocks = block_mask.shape[0]
    all_blocks = block_mask.shape[1]
    shaped = density.reshape(own_blocks, BS, all_blocks, BS)
    keeper = block_mask.astype(density.dtype)[:, None, :, None]
    return (shaped * keeper).reshape(density.shape)


def pair_routes(size):
    routes = []
    for dist in range(1, size // 2 + 1):
        if 2 * dist < size:
            route = [(r, (r + dist) % size) for r in range(size)]
        else:
            route = []
            for i in range(size // 2):
                if i % 2 == 0:
                    route.append((i, i + dist))
                else:
                    route.append((i + dist, i))
        recv_from = list(range(size))
        send_to = list(range(size))
        for src, dst in route:
            recv_from[dst] = src
            send_to[src] = dst
        routes.append((route, recv_from, send_to))
    return routes


def mask_slab(slab, live):
    keeper = jnp.repeat(jnp.repeat(live[:, 0, :].astype(slab.dtype), RB, axis=0), BS, axis=1)
    return slab * keeper[:, None, :]


def split_hi_lo(values):
    rounded = lax.reduce_precision(values, exponent_bits=8, mantissa_bits=7)
    return rounded.astype(jnp.bfloat16), (values - rounded).astype(jnp.bfloat16)


def weight_pair(values):
    hi, lo = split_hi_lo(values)
    both = jnp.stack([hi, lo])
    flat = both.transpose(2, 3, 0, 1).reshape(values.shape[1] * values.shape[2], -1)
    return with_layout_constraint(flat, Layout(major_to_minor=(0, 1)))


def slab_product(flat, weights):
    out = jnp.dot(flat, weights, preferred_element_type=jnp.float32)
    half = weights.shape[1] // 2
    return out[:, :half] + out[:, half:]


def add_cols(total, part, col_block):
    rows = part.shape[0]
    at = (jnp.int32(0), col_block * rows)
    here = lax.dynamic_slice(total, at, part.shape)
    return lax.dynamic_update_slice(total, here + part, at)


def per_device(tensor, live_blocks, occ_density, virt_density, occ_mask, virt_mask, pair_slots):
    rows = tensor.shape[0]
    assert tensor.shape[1] == BS
    planes = lax.axis_size("ri")
    cycle_size = lax.axis_size("ao")
    plane = lax.axis_index("ri")

    routes = pair_routes(planes)
    own = mask_slab(tensor, live_blocks)
    own_flat = own.reshape(rows, -1)
    lead = rows // 4
    early = [lax.ppermute(own_flat[:lead], "ri", route) for route, _, _ in routes]
    late = [lax.ppermute(own_flat[lead:], "ri", route) for route, _, _ in routes]

    stacked = jnp.stack(
        [screen_density(occ_density, occ_mask), screen_density(virt_density, virt_mask)]
    )
    full = lax.all_gather(stacked, "ao", axis=1, tiled=True)
    ao_total = full.shape[2]
    all_blocks = ao_total // BS
    picked = full.reshape(2, all_blocks, BS, ao_total)[:, pair_slots[0]]
    occ_rows = picked[0].reshape(KS * BS, ao_total)
    virt_rows = picked[1].reshape(KS * BS, ao_total)

    halves = jnp.einsum(
        "prk,dkc->cdrp",
        own,
        jnp.stack([occ_rows, virt_rows]),
        preferred_element_type=jnp.float32,
    ).astype(jnp.bfloat16)
    halves = with_layout_constraint(halves, Layout(major_to_minor=(0, 1, 2, 3)))
    halves, early = lax.optimization_barrier((halves, early))
    swapped = lax.all_to_all(halves, "ao", 0, 2, tiled=True)
    occ_t = swapped[:, 0]
    virt_t = swapped[:, 1]
    v_part = jnp.einsum("mn,lnp->plm", virt_rows, occ_t, preferred_element_type=jnp.float32)
    w_part = jnp.einsum("kl,nlq->qnk", occ_rows, virt_t, preferred_element_type=jnp.float32)
    v_weights = weight_pair(v_part)
    w_weights = weight_pair(w_part)
    early_stack = jnp.concatenate(early)
    early_mine = slab_product(early_stack, v_weights)
    with_own = slab_product(jnp.concatenate([own_flat, early_stack]), w_weights)
    diag = with_own[:rows]
    early_theirs = with_own[rows:]

    v_weights, w_weights, diag, early_mine, early_theirs, late = lax.optimization_barrier(
        (v_weights, w_weights, diag, early_mine, early_theirs, late)
    )
    late_stack = jnp.concatenate(late)
    late_mine = slab_product(late_stack, v_weights)
    late_theirs = slab_product(late_stack, w_weights)
    count = len(routes)
    lead = rows // 4
    rest = rows - lead

    def slab_rows(early_part, late_part, index):
        return jnp.concatenate(
            [early_part[index * lead:(index + 1) * lead], late_part[index * rest:(index + 1) * rest]]
        )

    mine_all = jnp.concatenate([slab_rows(early_mine, late_mine, i) for i in range(count)])
    theirs_all = jnp.concatenate([slab_rows(early_theirs, late_theirs, i) for i in range(count)])
    total = jnp.zeros((rows, planes * rows), jnp.float32)
    total = add_cols(total, diag, plane)
    for index, (route, recv_from, send_to) in enumerate(routes):
        source = jnp.array(recv_from, jnp.int32)[plane]
        target = jnp.array(send_to, jnp.int32)[plane]
        mine = mine_all[index * rows:(index + 1) * rows]
        theirs = theirs_all[index * rows:(index + 1) * rows]
        total = add_cols(total, mine.T, source)
        back = lax.ppermute(theirs, "ri", [(d, s) for s, d in route])
        total = add_cols(total, back, target)

    width = total.shape[1] // cycle_size
    sent = total.reshape(rows, cycle_size, width).transpose(1, 0, 2)
    got = lax.all_to_all(sent, "ao", 0, 0, tiled=True)
    return jnp.sum(got, axis=0)


def solution(mesh):
    placed = (
        P("ri", "ao", None),
        P("ri", "ao", None),
        P("ao", None),
        P("ao", None),
        P("ao", None),
        P("ao", None),
        P("ao", None),
    )
    return jax.shard_map(
        per_device, mesh=mesh, in_specs=placed, out_specs=P("ri", "ao"), check_vma=False
    )
```

```python
import jax
import jax.numpy as jnp
from jax import lax
from jax.experimental.layout import Layout, with_layout_constraint
from jax.sharding import PartitionSpec as P

BS = 32
KS = 8
RB = 64


def screen_density(density, block_mask):
    own_blocks = block_mask.shape[0]
    all_blocks = block_mask.shape[1]
    shaped = density.reshape(own_blocks, BS, all_blocks, BS)
    keeper = block_mask.astype(density.dtype)[:, None, :, None]
    return (shaped * keeper).reshape(density.shape)


def pair_routes(size):
    routes = []
    for dist in range(1, size // 2 + 1):
        if 2 * dist < size:
            route = [(r, (r + dist) % size) for r in range(size)]
        else:
            route = []
            for i in range(size // 2):
                if i % 2 == 0:
                    route.append((i, i + dist))
                else:
                    route.append((i + dist, i))
        recv_from = list(range(size))
        send_to = list(range(size))
        for src, dst in route:
            recv_from[dst] = src
            send_to[src] = dst
        routes.append((route, recv_from, send_to))
    return routes


def mask_slab(slab, live):
    keeper = jnp.repeat(jnp.repeat(live[:, 0, :].astype(slab.dtype), RB, axis=0), BS, axis=1)
    return slab * keeper[:, None, :]


def split_hi_lo(values):
    rounded = lax.reduce_precision(values, exponent_bits=8, mantissa_bits=7)
    return rounded.astype(jnp.bfloat16), (values - rounded).astype(jnp.bfloat16)


def weight_pair(values):
    hi, lo = split_hi_lo(values)
    both = jnp.stack([hi, lo])
    return both.transpose(2, 3, 0, 1).reshape(values.shape[1] * values.shape[2], -1)


def slab_product(flat, weights):
    out = jnp.dot(flat, weights, preferred_element_type=jnp.float32)
    half = weights.shape[1] // 2
    return out[:, :half] + out[:, half:]


def add_cols(total, part, col_block):
    rows = part.shape[0]
    at = (jnp.int32(0), col_block * rows)
    here = lax.dynamic_slice(total, at, part.shape)
    return lax.dynamic_update_slice(total, here + part, at)


def per_device(tensor, live_blocks, occ_density, virt_density, occ_mask, virt_mask, pair_slots):
    rows = tensor.shape[0]
    assert tensor.shape[1] == BS
    planes = lax.axis_size("ri")
    cycle_size = lax.axis_size("ao")
    plane = lax.axis_index("ri")

    routes = pair_routes(planes)
    own = mask_slab(tensor, live_blocks)
    own_flat = own.reshape(rows, -1)
    lead = rows // 4
    early = [lax.ppermute(own_flat[:lead], "ri", route) for route, _, _ in routes]
    late = [lax.ppermute(own_flat[lead:], "ri", route) for route, _, _ in routes]

    stacked = jnp.stack(
        [screen_density(occ_density, occ_mask), screen_density(virt_density, virt_mask)]
    )
    full = lax.all_gather(stacked, "ao", axis=1, tiled=True)
    ao_total = full.shape[2]
    all_blocks = ao_total // BS
    picked = full.reshape(2, all_blocks, BS, ao_total)[:, pair_slots[0]]
    occ_rows = picked[0].reshape(KS * BS, ao_total)
    virt_rows = picked[1].reshape(KS * BS, ao_total)

    occ_half = jnp.einsum(
        "prk,kc->crp", own, occ_rows, preferred_element_type=jnp.float32
    ).astype(jnp.bfloat16)
    virt_half = jnp.einsum(
        "prk,kc->crp", own, virt_rows, preferred_element_type=jnp.float32
    ).astype(jnp.bfloat16)
    row_major = Layout(major_to_minor=(0, 1, 2))
    occ_half = with_layout_constraint(occ_half, row_major)
    virt_half = with_layout_constraint(virt_half, row_major)
    occ_half, virt_half, early = lax.optimization_barrier((occ_half, virt_half, early))
    occ_t = lax.all_to_all(occ_half, "ao", 0, 1, tiled=True)
    virt_t = lax.all_to_all(virt_half, "ao", 0, 1, tiled=True)
    v_part = jnp.einsum("mn,lnp->plm", virt_rows, occ_t, preferred_element_type=jnp.float32)
    w_part = jnp.einsum("kl,nlq->qnk", occ_rows, virt_t, preferred_element_type=jnp.float32)
    v_weights = weight_pair(v_part)
    w_weights = weight_pair(w_part)
    early_stack = jnp.concatenate(early)
    early_mine = slab_product(early_stack, v_weights)
    with_own = slab_product(jnp.concatenate([own_flat, early_stack]), w_weights)
    diag = with_own[:rows]
    early_theirs = with_own[rows:]

    v_weights, w_weights, diag, early_mine, early_theirs, late = lax.optimization_barrier(
        (v_weights, w_weights, diag, early_mine, early_theirs, late)
    )
    late_stack = jnp.concatenate(late)
    late_mine = slab_product(late_stack, v_weights)
    late_theirs = slab_product(late_stack, w_weights)
    count = len(routes)
    lead = rows // 4
    rest = rows - lead

    def slab_rows(early_part, late_part, index):
        return jnp.concatenate(
            [early_part[index * lead:(index + 1) * lead], late_part[index * rest:(index + 1) * rest]]
        )

    mine_all = jnp.concatenate([slab_rows(early_mine, late_mine, i) for i in range(count)])
    theirs_all = jnp.concatenate([slab_rows(early_theirs, late_theirs, i) for i in range(count)])
    total = jnp.zeros((rows, planes * rows), jnp.float32)
    total = add_cols(total, diag, plane)
    for index, (route, recv_from, send_to) in enumerate(routes):
        source = jnp.array(recv_from, jnp.int32)[plane]
        target = jnp.array(send_to, jnp.int32)[plane]
        mine = mine_all[index * rows:(index + 1) * rows]
        theirs = theirs_all[index * rows:(index + 1) * rows]
        total = add_cols(total, mine.T, source)
        back = lax.ppermute(theirs, "ri", [(d, s) for s, d in route])
        total = add_cols(total, back, target)

    width = total.shape[1] // cycle_size
    sent = total.reshape(rows, cycle_size, width).transpose(1, 0, 2)
    got = lax.all_to_all(sent, "ao", 0, 0, tiled=True)
    return jnp.sum(got, axis=0)


def solution(mesh):
    placed = (
        P("ri", "ao", None),
        P("ri", "ao", None),
        P("ao", None),
        P("ao", None),
        P("ao", None),
        P("ao", None),
        P("ao", None),
    )
    return jax.shard_map(
        per_device, mesh=mesh, in_specs=placed, out_specs=P("ri", "ao"), check_vma=False
    )
```

```python
import jax
import jax.numpy as jnp
from jax import lax
from jax.experimental.layout import Layout, with_layout_constraint
from jax.sharding import PartitionSpec as P

BS = 32
KS = 8
RB = 64


def screen_density(density, block_mask):
    own_blocks = block_mask.shape[0]
    all_blocks = block_mask.shape[1]
    shaped = density.reshape(own_blocks, BS, all_blocks, BS)
    keeper = block_mask.astype(density.dtype)[:, None, :, None]
    return (shaped * keeper).reshape(density.shape)


def pair_routes(size):
    routes = []
    for dist in range(1, size // 2 + 1):
        if 2 * dist < size:
            route = [(r, (r + dist) % size) for r in range(size)]
        else:
            route = []
            for i in range(size // 2):
                if i % 2 == 0:
                    route.append((i, i + dist))
                else:
                    route.append((i + dist, i))
        recv_from = list(range(size))
        send_to = list(range(size))
        for src, dst in route:
            recv_from[dst] = src
            send_to[src] = dst
        routes.append((route, recv_from, send_to))
    return routes


def mask_slab(slab, live):
    keeper = jnp.repeat(jnp.repeat(live[:, 0, :].astype(slab.dtype), RB, axis=0), BS, axis=1)
    return slab * keeper[:, None, :]


def split_hi_lo(values):
    rounded = lax.reduce_precision(values, exponent_bits=8, mantissa_bits=7)
    return rounded.astype(jnp.bfloat16), (values - rounded).astype(jnp.bfloat16)


def weight_pair(values):
    hi, lo = split_hi_lo(values)
    both = jnp.stack([hi, lo])
    return both.transpose(2, 3, 0, 1).reshape(values.shape[1] * values.shape[2], -1)


def slab_product(flat, weights):
    out = jnp.dot(flat, weights, preferred_element_type=jnp.float32)
    half = weights.shape[1] // 2
    return out[:, :half] + out[:, half:]


def add_cols(total, part, col_block):
    rows = part.shape[0]
    at = (jnp.int32(0), col_block * rows)
    here = lax.dynamic_slice(total, at, part.shape)
    return lax.dynamic_update_slice(total, here + part, at)


def per_device(tensor, live_blocks, occ_density, virt_density, occ_mask, virt_mask, pair_slots):
    rows = tensor.shape[0]
    assert tensor.shape[1] == BS
    planes = lax.axis_size("ri")
    cycle_size = lax.axis_size("ao")
    plane = lax.axis_index("ri")

    routes = pair_routes(planes)
    own = mask_slab(tensor, live_blocks)
    own_flat = own.reshape(rows, -1)
    lead = rows * 5 // 16
    early = [lax.ppermute(own_flat[:lead], "ri", route) for route, _, _ in routes]
    late = [lax.ppermute(own_flat[lead:], "ri", route) for route, _, _ in routes]

    stacked = jnp.stack(
        [screen_density(occ_density, occ_mask), screen_density(virt_density, virt_mask)]
    )
    full = lax.all_gather(stacked, "ao", axis=1, tiled=True)
    ao_total = full.shape[2]
    all_blocks = ao_total // BS
    picked = full.reshape(2, all_blocks, BS, ao_total)[:, pair_slots[0]]
    occ_rows = picked[0].reshape(KS * BS, ao_total)
    virt_rows = picked[1].reshape(KS * BS, ao_total)

    halves = jnp.einsum(
        "prk,dkc->cdrp",
        own,
        jnp.stack([occ_rows, virt_rows]),
        preferred_element_type=jnp.float32,
    ).astype(jnp.bfloat16)
    halves = with_layout_constraint(halves, Layout(major_to_minor=(0, 1, 2, 3)))
    halves, early = lax.optimization_barrier((halves, early))
    swapped = lax.all_to_all(halves, "ao", 0, 2, tiled=True)
    occ_t = swapped[:, 0]
    virt_t = swapped[:, 1]
    v_part = jnp.einsum("mn,lnp->plm", virt_rows, occ_t, preferred_element_type=jnp.float32)
    w_part = jnp.einsum("kl,nlq->qnk", occ_rows, virt_t, preferred_element_type=jnp.float32)
    v_weights = weight_pair(v_part)
    w_weights = weight_pair(w_part)
    early_stack = jnp.concatenate(early)
    early_mine = slab_product(early_stack, v_weights)
    with_own = slab_product(jnp.concatenate([own_flat, early_stack]), w_weights)
    diag = with_own[:rows]
    early_theirs = with_own[rows:]

    v_weights, w_weights, diag, early_mine, early_theirs, late = lax.optimization_barrier(
        (v_weights, w_weights, diag, early_mine, early_theirs, late)
    )
    late_stack = jnp.concatenate(late)
    late_mine = slab_product(late_stack, v_weights)
    late_theirs = slab_product(late_stack, w_weights)
    count = len(routes)
    lead = rows * 5 // 16
    rest = rows - lead

    def slab_rows(early_part, late_part, index):
        return jnp.concatenate(
            [early_part[index * lead:(index + 1) * lead], late_part[index * rest:(index + 1) * rest]]
        )

    mine_all = jnp.concatenate([slab_rows(early_mine, late_mine, i) for i in range(count)])
    theirs_all = jnp.concatenate([slab_rows(early_theirs, late_theirs, i) for i in range(count)])
    total = jnp.zeros((rows, planes * rows), jnp.float32)
    total = add_cols(total, diag, plane)
    for index, (route, recv_from, send_to) in enumerate(routes):
        source = jnp.array(recv_from, jnp.int32)[plane]
        target = jnp.array(send_to, jnp.int32)[plane]
        mine = mine_all[index * rows:(index + 1) * rows]
        theirs = theirs_all[index * rows:(index + 1) * rows]
        total = add_cols(total, mine.T, source)
        back = lax.ppermute(theirs, "ri", [(d, s) for s, d in route])
        total = add_cols(total, back, target)

    width = total.shape[1] // cycle_size
    sent = total.reshape(rows, cycle_size, width).transpose(1, 0, 2)
    got = lax.all_to_all(sent, "ao", 0, 0, tiled=True)
    return jnp.sum(got, axis=0)


def solution(mesh):
    placed = (
        P("ri", "ao", None),
        P("ri", "ao", None),
        P("ao", None),
        P("ao", None),
        P("ao", None),
        P("ao", None),
        P("ao", None),
    )
    return jax.shard_map(
        per_device, mesh=mesh, in_specs=placed, out_specs=P("ri", "ao"), check_vma=False
    )
```
